128 devices in a mesh: wide: 32 (over y, x, z_lo), narrow: 4 (over z_hi, core).
Axes of the slice: x: 4, y: 4, z: 4 (z_hi: 2, z_lo: 2; z = z_hi * 2 + z_lo), core: 2. Of those that a mesh axis runs over, the one named last changes fastest.
Arguments:
- sources: int32 [256, 256, 256], P('wide', 'narrow'), may hold values from 0 to 1
- labels: int32 [256, 256, 256], P('wide', 'narrow'), may hold values from 0 to 1, as said below
Outputs:
- distance: float32 [256, 256, 256], P('wide', 'narrow')
The draws below stay inside these ranges and needn't reach their ends.
Inputs may be any that keep to these rules, and one draw needn't show every extreme that they name: labels marks the union of several periodic balls of radii between 16 and 42 cells; sources marks exactly the labelled cells that have an unlabelled neighbour along one of the six grid directions.
All inputs are finite; a program needn't handle non-finite values.
Results may differ from the reference program's by a relative error of at most 0.00022.
Values sent between devices are 32-bit elements; how exact they have to be, the bound alone decides.
No kernel may reach another device: no remote copies, remote signals or barrier semaphores. Data moves between devices by JAX's collectives and lax.ppermute only.
A program may use at most 128 MiB of HBM per device.

```python
import math
import jax
import jax.numpy as jnp

G = 256


def ball_union(key):
    inner = jax.random.fold_in(key, 7)
    key_centers, key_radii = jax.random.split(inner)
    centers = jax.random.randint(key_centers, (8, 3), 0, G, dtype=jnp.int32)
    radii = jax.random.randint(key_radii, (8,), G // 16, G // 6 + 1, dtype=jnp.int32)
    positions = jnp.arange(G, dtype=jnp.int32)
    inside = jnp.zeros((G, G, G), dtype=jnp.bool_)
    for ball in range(8):
        offset_x = (positions - centers[ball, 0] + G // 2) % G - G // 2
        offset_y = (positions - centers[ball, 1] + G // 2) % G - G // 2
        offset_z = (positions - centers[ball, 2] + G // 2) % G - G // 2
        square = (offset_x * offset_x)[:, None, None] + (offset_y * offset_y)[None, :, None] + (offset_z * offset_z)[None, None, :]
        inside = inside | (square <= radii[ball] * radii[ball])
    return inside


def draw_labels(key, part):
    return ball_union(key).astype(jnp.int32)


def draw_sources(key, part):
    inside = ball_union(key)
    outside_near = jnp.zeros_like(inside)
    for dimension in range(3):
        outside_near = outside_near | jnp.logical_not(jnp.roll(inside, 1, dimension))
        outside_near = outside_near | jnp.logical_not(jnp.roll(inside, -1, dimension))
    return (inside & outside_near).astype(jnp.int32)


def setup_inputs(seed: int = 0) -> dict:
    arg_keys = jax.random.split(jax.random.key(seed), 3)
    return {
        "sources": draw_sources(jax.random.fold_in(arg_keys[2], 71), 0),
        "labels": draw_labels(jax.random.fold_in(arg_keys[2], 71), 0),
    }


def wave_terms(length):
    positions = jnp.arange(length, dtype=jnp.int32).astype(jnp.float32)
    angles = positions * (2.0 * math.pi / length)
    return (2.0 - 2.0 * jnp.cos(angles), jnp.sin(angles))

def central(values, dimension):
    return 0.5 * (jnp.roll(values, -1, dimension) - jnp.roll(values, 1, dimension))

def reference(sources, labels):
    heat_time = (G / 8.0) ** 2
    grad_floor = 0.04 / heat_time
    source = sources.astype(jnp.float32)
    eigenvalue, sine_wave = wave_terms(G)
    laplace = eigenvalue[:, None, None] + eigenvalue[None, :, None] + eigenvalue[None, None, :]
    spectrum = jnp.fft.fftn(source)
    heat_field = jnp.real(jnp.fft.ifftn(spectrum / (1.0 + heat_time * laplace))).astype(jnp.float32)
    grad_x = central(heat_field, 0)
    grad_y = central(heat_field, 1)
    grad_z = central(heat_field, 2)
    magnitude = jnp.sqrt(grad_x * grad_x + grad_y * grad_y + grad_z * grad_z)
    limited = jnp.maximum(magnitude, grad_floor)
    flow_x = -grad_x / limited
    flow_y = -grad_y / limited
    flow_z = -grad_z / limited
    divergence = central(flow_x, 0) + central(flow_y, 1) + central(flow_z, 2)
    laplace_safe = laplace.at[0, 0, 0].set(1.0)
    potential_hat = -jnp.fft.fftn(divergence) / laplace_safe
    potential_hat = potential_hat.at[0, 0, 0].set(0.0)
    potential = jnp.real(jnp.fft.ifftn(potential_hat)).astype(jnp.float32)
    signs = (2 * labels - 1).astype(jnp.float32)
    return signs * potential
```

```python
import math

import jax
import jax.numpy as jnp
from jax import lax
from jax.sharding import PartitionSpec as P

highest = lax.Precision.HIGHEST


def cas_table(length):
    positions = jnp.arange(length, dtype=jnp.int32)
    phase_steps = positions[:, None] * positions[None, :] % length
    angles = phase_steps.astype(jnp.float32) * (2.0 * math.pi / length)
    return jnp.cos(angles) + jnp.sin(angles)


def eigen(wavenumber, length):
    angles = wavenumber.astype(jnp.float32) * (2.0 * math.pi / length)
    return 2.0 - 2.0 * jnp.cos(angles)


def forward(values, cas):
    along_z = jnp.einsum("xyz,zk->xyk", values, cas, precision=highest)
    arrived = lax.all_to_all(along_z, "narrow", 2, 1, tiled=True)
    along_y = jnp.einsum("xyk,yl->xlk", arrived, cas, precision=highest)
    arrived = lax.all_to_all(along_y, "wide", 1, 0, tiled=True)
    return jnp.einsum("xlk,xm->mlk", arrived, cas, precision=highest)


def inverse(spectrum, cas):
    along_x = jnp.einsum("mlk,mx->xlk", spectrum, cas, precision=highest)
    arrived = lax.all_to_all(along_x, "wide", 0, 1, tiled=True)
    along_y = jnp.einsum("xlk,ly->xyk", arrived, cas, precision=highest)
    arrived = lax.all_to_all(along_y, "narrow", 1, 2, tiled=True)
    return jnp.einsum("xyk,kz->xyz", arrived, cas, precision=highest)


def from_neighbour(values, axis_name, offset):
    size = lax.axis_size(axis_name)
    return lax.ppermute(values, axis_name, [((i + offset) % size, i) for i in range(size)])


def with_halo(values, axis, axis_name, width):
    count = values.shape[axis]
    low = lax.slice_in_dim(values, count - width, count, axis=axis)
    high = lax.slice_in_dim(values, 0, width, axis=axis)
    return jnp.concatenate(
        (from_neighbour(low, axis_name, -1), values, from_neighbour(high, axis_name, 1)), axis=axis
    )


def central_z(values):
    return 0.5 * (jnp.roll(values, -1, 2) - jnp.roll(values, 1, 2))


def divergence_of_flow(heat, grad_floor):
    count_x = heat.shape[0] - 4
    count_y = heat.shape[1] - 4
    inner = heat[1:-1, 1:-1]
    grad_x = 0.5 * (heat[2:, 1:-1] - heat[:-2, 1:-1])
    grad_y = 0.5 * (heat[1:-1, 2:] - heat[1:-1, :-2])
    grad_z = central_z(inner)
    magnitude = jnp.sqrt(grad_x * grad_x + grad_y * grad_y + grad_z * grad_z)
    limited = jnp.maximum(magnitude, grad_floor)
    flow_x = -grad_x / limited
    flow_y = -grad_y / limited
    flow_z = -grad_z / limited
    div_x = 0.5 * (flow_x[2:, 1:-1] - flow_x[:-2, 1:-1])
    div_y = 0.5 * (flow_y[1:-1, 2:] - flow_y[1:-1, :-2])
    div_z = central_z(flow_z[1:-1, 1:-1])
    assert div_x.shape[:2] == (count_x, count_y)
    return div_x + div_y + div_z


def per_device(sources, labels):
    length = sources.shape[2]
    heat_time = (length / 8.0) ** 2
    grad_floor = 0.04 / heat_time
    scale = 1.0 / float(length) ** 3
    cas = cas_table(length)
    span_wide = length // lax.axis_size("wide")
    span_narrow = length // lax.axis_size("narrow")
    wave_x = jnp.arange(length, dtype=jnp.int32)
    wave_y = lax.axis_index("wide") * span_wide + jnp.arange(span_wide, dtype=jnp.int32)
    wave_z = lax.axis_index("narrow") * span_narrow + jnp.arange(span_narrow, dtype=jnp.int32)
    laplace = (
        eigen(wave_x, length)[:, None, None] + eigen(wave_y, length)[None, :, None]
    ) + eigen(wave_z, length)[None, None, :]
    anchor = (
        (wave_x[:, None, None] == 0) & (wave_y[None, :, None] == 0) & (wave_z[None, None, :] == 0)
    )

    source = sources.astype(jnp.float32)
    spectrum = forward(source, cas)
    heat = inverse(spectrum / (1.0 + heat_time * laplace) * scale, cas)

    padded = with_halo(with_halo(heat, 0, "wide", 2), 1, "narrow", 2)
    divergence = divergence_of_flow(padded, grad_floor)

    div_spectrum = forward(divergence, cas)
    laplace_safe = jnp.where(anchor, 1.0, laplace)
    potential_spectrum = jnp.where(anchor, 0.0, -div_spectrum / laplace_safe) * scale
    potential = inverse(potential_spectrum, cas)
    signs = (2 * labels - 1).astype(jnp.float32)
    return signs * potential


def solution(mesh):
    return jax.shard_map(
        per_device,
        mesh=mesh,
        in_specs=(P("wide", "narrow", None), P("wide", "narrow", None)),
        out_specs=P("wide", "narrow", None),
        check_vma=False,
    )
```

```python
import math

import jax
import jax.numpy as jnp
from jax import lax
from jax.sharding import PartitionSpec as P

highest = lax.Precision.HIGHEST
ALL = ("wide", "narrow")


def cas_table(length):
    positions = jnp.arange(length, dtype=jnp.int32)
    phase_steps = positions[:, None] * positions[None, :] % length
    angles = phase_steps.astype(jnp.float32) * (2.0 * math.pi / length)
    return jnp.cos(angles) + jnp.sin(angles)


def eigen(wavenumber, length):
    angles = wavenumber.astype(jnp.float32) * (2.0 * math.pi / length)
    return 2.0 - 2.0 * jnp.cos(angles)


def to_pencil(slab, cas):
    rows, length, _ = slab.shape
    devices = lax.axis_size(ALL)
    span = length // devices
    send = slab.reshape(rows, devices, span, length).transpose(1, 0, 2, 3)
    arrived = lax.all_to_all(send, ALL, 0, 0)
    return jnp.einsum("sxyk,sxm->myk", arrived, cas.reshape(devices, rows, length), precision=highest)


def to_slab(pencil, cas):
    length, span, _ = pencil.shape
    devices = lax.axis_size(ALL)
    rows = length // devices
    along_x = jnp.einsum("myk,mx->xyk", pencil, cas, precision=highest)
    arrived = lax.all_to_all(along_x.reshape(devices, rows, span, length), ALL, 0, 0)
    return jnp.einsum("sxyk,syl->xlk", arrived, cas.reshape(devices, span, length), precision=highest)


def plane_forward(slab, cas):
    along_z = jnp.einsum("xyz,zk->xyk", slab, cas, precision=highest)
    return jnp.einsum("xyk,yl->xlk", along_z, cas, precision=highest)


def from_neighbour(values, offset):
    size = lax.axis_size(ALL)
    return lax.ppermute(values, ALL, [((i + offset) % size, i) for i in range(size)])


def central(values, axis):
    return 0.5 * (jnp.roll(values, -1, axis) - jnp.roll(values, 1, axis))


def divergence_of_flow(heat, grad_floor):
    inner = heat[1:-1]
    grad_x = 0.5 * (heat[2:] - heat[:-2])
    grad_y = central(inner, 1)
    grad_z = central(inner, 2)
    magnitude = jnp.sqrt(grad_x * grad_x + grad_y * grad_y + grad_z * grad_z)
    limited = jnp.maximum(magnitude, grad_floor)
    flow_x = -grad_x / limited
    flow_y = -grad_y / limited
    flow_z = -grad_z / limited
    div_x = 0.5 * (flow_x[2:] - flow_x[:-2])
    return div_x + central(flow_y[1:-1], 1) + central(flow_z[1:-1], 2)


def per_device(sources, labels):
    count_x, count_y, length = sources.shape
    narrow = lax.axis_size("narrow")
    devices = lax.axis_size(ALL)
    rows = count_x // narrow
    span = length // devices
    heat_time = (length / 8.0) ** 2
    grad_floor = 0.04 / heat_time
    scale = 1.0 / float(length) ** 3
    cas = cas_table(length)
    wave = jnp.arange(length, dtype=jnp.int32)
    wave_y = lax.axis_index(ALL) * span + jnp.arange(span, dtype=jnp.int32)
    laplace = (
        eigen(wave, length)[:, None, None] + eigen(wave_y, length)[None, :, None]
    ) + eigen(wave, length)[None, None, :]
    anchor = (wave[:, None, None] == 0) & (wave_y[None, :, None] == 0) & (wave[None, None, :] == 0)

    source = sources.astype(jnp.float32).reshape(narrow, rows, count_y, length)
    arrived = lax.all_to_all(source, "narrow", 0, 0)
    along_z = jnp.einsum("sxyz,zk->sxyk", arrived, cas, precision=highest)
    planes = jnp.einsum("sxyk,syl->xlk", along_z, cas.reshape(narrow, count_y, length), precision=highest)

    spectrum = to_pencil(planes, cas)
    heat_planes = to_slab(spectrum / (1.0 + heat_time * laplace) * scale, cas)
    heat = jnp.einsum("xyk,kz->xyz", heat_planes, cas, precision=highest)

    padded = jnp.concatenate((from_neighbour(heat[-2:], -1), heat, from_neighbour(heat[:2], 1)), axis=0)
    divergence = divergence_of_flow(padded, grad_floor)

    div_spectrum = to_pencil(plane_forward(divergence, cas), cas)
    laplace_safe = jnp.where(anchor, 1.0, laplace)
    potential_spectrum = jnp.where(anchor, 0.0, -div_spectrum / laplace_safe) * scale
    potential = jnp.einsum("xyk,kz->xyz", to_slab(potential_spectrum, cas), cas, precision=highest)

    send = potential.reshape(rows, narrow, count_y, length).transpose(1, 0, 2, 3)
    arrived = lax.all_to_all(send, "narrow", 0, 0).reshape(count_x, count_y, length)
    signs = (2 * labels - 1).astype(jnp.float32)
    return signs * arrived


def solution(mesh):
    return jax.shard_map(
        per_device,
        mesh=mesh,
        in_specs=(P("wide", "narrow", None), P("wide", "narrow", None)),
        out_specs=P("wide", "narrow", None),
        check_vma=False,
    )
```

```python
import math

import jax
import jax.numpy as jnp
from jax import lax
from jax.sharding import PartitionSpec as P

highest = lax.Precision.HIGHEST
ALL = ("wide", "narrow")


def cas_table(length):
    positions = jnp.arange(length, dtype=jnp.int32)
    phase_steps = positions[:, None] * positions[None, :] % length
    angles = phase_steps.astype(jnp.float32) * (2.0 * math.pi / length)
    return jnp.cos(angles) + jnp.sin(angles)


def eigen(wavenumber, length):
    angles = wavenumber.astype(jnp.float32) * (2.0 * math.pi / length)
    return 2.0 - 2.0 * jnp.cos(angles)


def to_planes(pencil, cas):
    count_x, count_y, length = pencil.shape
    wide = lax.axis_size("wide")
    narrow = lax.axis_size("narrow")
    span = length // (wide * narrow)
    along_z = jnp.einsum("xyz,zk->kxy", pencil, cas, precision=highest)
    arrived = lax.all_to_all(along_z.reshape(wide * narrow, span, count_x, count_y), ALL, 0, 0)
    arrived = arrived.reshape(wide, narrow, span, count_x, count_y).transpose(2, 0, 3, 1, 4)
    return arrived.reshape(span, wide * count_x, narrow * count_y)


def to_pencil(planes, cas, count_x, count_y):
    span, _, _ = planes.shape
    wide = lax.axis_size("wide")
    narrow = lax.axis_size("narrow")
    send = planes.reshape(span, wide, count_x, narrow, count_y).transpose(1, 3, 0, 2, 4)
    arrived = lax.all_to_all(send.reshape(wide * narrow, span, count_x, count_y), ALL, 0, 0)
    spectrum = arrived.reshape(wide * narrow * span, count_x, count_y)
    return jnp.einsum("kxy,kz->xyz", spectrum, cas, precision=highest)


def planes_forward(planes, cas):
    along_y = jnp.einsum("kxy,yl->kxl", planes, cas, precision=highest)
    return jnp.einsum("kxl,xm->kml", along_y, cas, precision=highest)


def planes_inverse(spectrum, cas):
    along_x = jnp.einsum("kml,mx->kxl", spectrum, cas, precision=highest)
    return jnp.einsum("kxl,ly->kxy", along_x, cas, precision=highest)


def from_neighbour(values, axis_name, offset):
    size = lax.axis_size(axis_name)
    return lax.ppermute(values, axis_name, [((i + offset) % size, i) for i in range(size)])


def with_halo(values, axis, axis_name, width):
    count = values.shape[axis]
    low = lax.slice_in_dim(values, count - width, count, axis=axis)
    high = lax.slice_in_dim(values, 0, width, axis=axis)
    return jnp.concatenate(
        (from_neighbour(low, axis_name, -1), values, from_neighbour(high, axis_name, 1)), axis=axis
    )


def central_z(values):
    return 0.5 * (jnp.roll(values, -1, 2) - jnp.roll(values, 1, 2))


def divergence_of_flow(heat, grad_floor):
    inner = heat[1:-1, 1:-1]
    grad_x = 0.5 * (heat[2:, 1:-1] - heat[:-2, 1:-1])
    grad_y = 0.5 * (heat[1:-1, 2:] - heat[1:-1, :-2])
    grad_z = central_z(inner)
    magnitude = jnp.sqrt(grad_x * grad_x + grad_y * grad_y + grad_z * grad_z)
    limited = jnp.maximum(magnitude, grad_floor)
    flow_x = -grad_x / limited
    flow_y = -grad_y / limited
    flow_z = -grad_z / limited
    div_x = 0.5 * (flow_x[2:, 1:-1] - flow_x[:-2, 1:-1])
    div_y = 0.5 * (flow_y[1:-1, 2:] - flow_y[1:-1, :-2])
    div_z = central_z(flow_z[1:-1, 1:-1])
    return div_x + div_y + div_z


def per_device(sources, labels):
    count_x, count_y, length = sources.shape
    span = length // lax.axis_size(ALL)
    heat_time = (length / 8.0) ** 2
    grad_floor = 0.04 / heat_time
    scale = 1.0 / float(length) ** 3
    cas = cas_table(length)
    wave = jnp.arange(length, dtype=jnp.int32)
    wave_z = lax.axis_index(ALL) * span + jnp.arange(span, dtype=jnp.int32)
    laplace = (
        eigen(wave, length)[None, :, None] + eigen(wave, length)[None, None, :]
    ) + eigen(wave_z, length)[:, None, None]
    anchor = (wave_z[:, None, None] == 0) & (wave[None, :, None] == 0) & (wave[None, None, :] == 0)

    source = sources.astype(jnp.float32)
    spectrum = planes_forward(to_planes(source, cas), cas)
    heat_planes = planes_inverse(spectrum / (1.0 + heat_time * laplace) * scale, cas)
    heat = to_pencil(heat_planes, cas, count_x, count_y)

    padded = with_halo(with_halo(heat, 0, "wide", 2), 1, "narrow", 2)
    divergence = divergence_of_flow(padded, grad_floor)

    div_spectrum = planes_forward(to_planes(divergence, cas), cas)
    laplace_safe = jnp.where(anchor, 1.0, laplace)
    potential_spectrum = jnp.where(anchor, 0.0, -div_spectrum / laplace_safe) * scale
    potential = to_pencil(planes_inverse(potential_spectrum, cas), cas, count_x, count_y)
    signs = (2 * labels - 1).astype(jnp.float32)
    return signs * potential


def solution(mesh):
    return jax.shard_map(
        per_device,
        mesh=mesh,
        in_specs=(P("wide", "narrow", None), P("wide", "narrow", None)),
        out_specs=P("wide", "narrow", None),
        check_vma=False,
    )
```

```python
import math

import jax
import jax.numpy as jnp
from jax import lax
from jax.sharding import PartitionSpec as P

highest = lax.Precision.HIGHEST
ALL = ("wide", "narrow")


def cas_table(length):
    positions = jnp.arange(length, dtype=jnp.int32)
    phase_steps = positions[:, None] * positions[None, :] % length
    angles = phase_steps.astype(jnp.float32) * (2.0 * math.pi / length)
    return jnp.cos(angles) + jnp.sin(angles)


def eigen(wavenumber, length):
    angles = wavenumber.astype(jnp.float32) * (2.0 * math.pi / length)
    return 2.0 - 2.0 * jnp.cos(angles)


def to_planes(pencil, cas):
    count_x, count_y, length = pencil.shape
    wide = lax.axis_size("wide")
    narrow = lax.axis_size("narrow")
    span = length // (wide * narrow)
    along_z = jnp.einsum("xyz,zk->kxy", pencil, cas, precision=highest)
    arrived = lax.all_to_all(along_z.reshape(wide * narrow, span, count_x, count_y), ALL, 0, 0)
    arrived = arrived.reshape(wide, narrow, span, count_x, count_y).transpose(2, 0, 3, 1, 4)
    return arrived.reshape(span, wide * count_x, narrow * count_y)


def to_pencil(planes, cas, count_x, count_y):
    span, _, _ = planes.shape
    wide = lax.axis_size("wide")
    narrow = lax.axis_size("narrow")
    send = planes.reshape(span, wide, count_x, narrow, count_y).transpose(1, 3, 0, 2, 4)
    arrived = lax.all_to_all(send.reshape(wide * narrow, span, count_x, count_y), ALL, 0, 0)
    spectrum = arrived.reshape(wide * narrow * span, count_x, count_y)
    return jnp.einsum("kxy,kz->xyz", spectrum, cas, precision=highest)


def planes_forward(planes, cas):
    along_y = jnp.einsum("kxy,yl->kxl", planes, cas, precision=highest)
    return jnp.einsum("kxl,xm->kml", along_y, cas, precision=highest)


def planes_inverse(spectrum, cas):
    along_x = jnp.einsum("kml,mx->kxl", spectrum, cas, precision=highest)
    return jnp.einsum("kxl,ly->kxy", along_x, cas, precision=highest)


def from_neighbour(values, axis_name, offset):
    size = lax.axis_size(axis_name)
    return lax.ppermute(values, axis_name, [((i + offset) % size, i) for i in range(size)])


def with_halo(values, axis, axis_name, width):
    count = values.shape[axis]
    low = lax.slice_in_dim(values, count - width, count, axis=axis)
    high = lax.slice_in_dim(values, 0, width, axis=axis)
    return jnp.concatenate(
        (from_neighbour(low, axis_name, -1), values, from_neighbour(high, axis_name, 1)), axis=axis
    )


def central_z(values):
    return 0.5 * (jnp.roll(values, -1, 2) - jnp.roll(values, 1, 2))


def divergence_of_flow(heat, grad_floor):
    inner = heat[1:-1, 1:-1]
    grad_x = 0.5 * (heat[2:, 1:-1] - heat[:-2, 1:-1])
    grad_y = 0.5 * (heat[1:-1, 2:] - heat[1:-1, :-2])
    grad_z = central_z(inner)
    magnitude = jnp.sqrt(grad_x * grad_x + grad_y * grad_y + grad_z * grad_z)
    limited = jnp.maximum(magnitude, grad_floor)
    flow_x = -grad_x / limited
    flow_y = -grad_y / limited
    flow_z = -grad_z / limited
    div_x = 0.5 * (flow_x[2:, 1:-1] - flow_x[:-2, 1:-1])
    div_y = 0.5 * (flow_y[1:-1, 2:] - flow_y[1:-1, :-2])
    div_z = central_z(flow_z[1:-1, 1:-1])
    return div_x + div_y + div_z


def per_device(sources, labels):
    count_x, count_y, length = sources.shape
    span = length // lax.axis_size(ALL)
    heat_time = (length / 8.0) ** 2
    grad_floor = 0.04 / heat_time
    scale = 1.0 / float(length) ** 3
    cas = cas_table(length)
    wave = jnp.arange(length, dtype=jnp.int32)
    wave_z = lax.axis_index(ALL) * span + jnp.arange(span, dtype=jnp.int32)
    laplace = (
        eigen(wave, length)[None, :, None] + eigen(wave, length)[None, None, :]
    ) + eigen(wave_z, length)[:, None, None]
    anchor = (wave_z[:, None, None] == 0) & (wave[None, :, None] == 0) & (wave[None, None, :] == 0)

    heat_filter = 1.0 + heat_time * laplace
    laplace_safe = jnp.where(anchor, 1.0, laplace)
    source, heat_filter, laplace_safe, anchor = lax.optimization_barrier(
        (sources.astype(jnp.float32), heat_filter, laplace_safe, anchor)
    )
    spectrum = planes_forward(to_planes(source, cas), cas)
    heat_planes = planes_inverse(spectrum / heat_filter * scale, cas)
    heat = to_pencil(heat_planes, cas, count_x, count_y)

    padded = with_halo(with_halo(heat, 0, "wide", 2), 1, "narrow", 2)
    divergence = divergence_of_flow(padded, grad_floor)

    div_spectrum = planes_forward(to_planes(divergence, cas), cas)
    potential_spectrum = jnp.where(anchor, 0.0, -div_spectrum / laplace_safe) * scale
    potential = to_pencil(planes_inverse(potential_spectrum, cas), cas, count_x, count_y)
    signs = (2 * labels - 1).astype(jnp.float32)
    return signs * potential


def solution(mesh):
    return jax.shard_map(
        per_device,
        mesh=mesh,
        in_specs=(P("wide", "narrow", None), P("wide", "narrow", None)),
        out_specs=P("wide", "narrow", None),
        check_vma=False,
    )
```

```python
import math

import jax
import jax.numpy as jnp
from jax import lax
from jax.sharding import PartitionSpec as P

highest = lax.Precision.HIGHEST
ALL = ("wide", "narrow")


def cas_table(length):
    positions = jnp.arange(length, dtype=jnp.int32)
    phase_steps = positions[:, None] * positions[None, :] % length
    angles = phase_steps.astype(jnp.float32) * (2.0 * math.pi / length)
    return jnp.cos(angles) + jnp.sin(angles)


def eigen(wavenumber, length):
    angles = wavenumber.astype(jnp.float32) * (2.0 * math.pi / length)
    return 2.0 - 2.0 * jnp.cos(angles)


def to_planes(pencil, cas):
    count_x, count_y, length = pencil.shape
    wide = lax.axis_size("wide")
    narrow = lax.axis_size("narrow")
    span = length // (wide * narrow)
    along_z = jnp.einsum("xyz,zk->kxy", pencil, cas, precision=highest)
    arrived = lax.all_to_all(along_z.reshape(wide * narrow, span, count_x, count_y), ALL, 0, 0)
    arrived = arrived.reshape(wide, narrow, span, count_x, count_y).transpose(2, 0, 3, 1, 4)
    return arrived.reshape(span, wide * count_x, narrow * count_y)


def to_pencil(planes, cas, count_x, count_y):
    span, _, _ = planes.shape
    wide = lax.axis_size("wide")
    narrow = lax.axis_size("narrow")
    send = planes.reshape(span, wide, count_x, narrow, count_y).transpose(1, 3, 0, 2, 4)
    arrived = lax.all_to_all(send.reshape(wide * narrow, span, count_x, count_y), ALL, 0, 0)
    spectrum = arrived.reshape(wide * narrow * span, count_x, count_y)
    return jnp.einsum("kxy,kz->xyz", spectrum, cas, precision=highest)


def planes_forward(planes, cas):
    along_y = jnp.einsum("kxy,yl->kxl", planes, cas, precision=highest)
    return jnp.einsum("kxl,xm->kml", along_y, cas, precision=highest)


def planes_inverse(spectrum, cas):
    along_x = jnp.einsum("kml,mx->kxl", spectrum, cas, precision=highest)
    return jnp.einsum("kxl,ly->kxy", along_x, cas, precision=highest)


def from_offset(values, offset_wide, offset_narrow):
    wide = lax.axis_size("wide")
    narrow = lax.axis_size("narrow")
    pairs = []
    for w in range(wide):
        for q in range(narrow):
            source = ((w + offset_wide) % wide) * narrow + (q + offset_narrow) % narrow
            pairs.append((source, w * narrow + q))
    return lax.ppermute(values, ALL, pairs)


def with_halo(values, width):
    low_x, high_x = values[-width:], values[:width]
    pieces = {}
    for offset_wide, rows in ((-1, low_x), (0, values), (1, high_x)):
        for offset_narrow, take in ((-1, slice(-width, None)), (0, slice(None)), (1, slice(0, width))):
            block = rows[:, take]
            if offset_wide or offset_narrow:
                block = from_offset(block, offset_wide, offset_narrow)
            pieces[offset_wide, offset_narrow] = block
    bands = [
        jnp.concatenate([pieces[offset_wide, offset_narrow] for offset_narrow in (-1, 0, 1)], axis=1)
        for offset_wide in (-1, 0, 1)
    ]
    return jnp.concatenate(bands, axis=0)


def central_z(values):
    return 0.5 * (jnp.roll(values, -1, 2) - jnp.roll(values, 1, 2))


def divergence_of_flow(heat, grad_floor):
    inner = heat[1:-1, 1:-1]
    grad_x = 0.5 * (heat[2:, 1:-1] - heat[:-2, 1:-1])
    grad_y = 0.5 * (heat[1:-1, 2:] - heat[1:-1, :-2])
    grad_z = central_z(inner)
    magnitude = jnp.sqrt(grad_x * grad_x + grad_y * grad_y + grad_z * grad_z)
    limited = jnp.maximum(magnitude, grad_floor)
    flow_x = -grad_x / limited
    flow_y = -grad_y / limited
    flow_z = -grad_z / limited
    div_x = 0.5 * (flow_x[2:, 1:-1] - flow_x[:-2, 1:-1])
    div_y = 0.5 * (flow_y[1:-1, 2:] - flow_y[1:-1, :-2])
    div_z = central_z(flow_z[1:-1, 1:-1])
    return div_x + div_y + div_z


def per_device(sources, labels):
    count_x, count_y, length = sources.shape
    span = length // lax.axis_size(ALL)
    heat_time = (length / 8.0) ** 2
    grad_floor = 0.04 / heat_time
    scale = 1.0 / float(length) ** 3
    cas = cas_table(length)
    wave = jnp.arange(length, dtype=jnp.int32)
    wave_z = lax.axis_index(ALL) * span + jnp.arange(span, dtype=jnp.int32)
    laplace = (
        eigen(wave, length)[None, :, None] + eigen(wave, length)[None, None, :]
    ) + eigen(wave_z, length)[:, None, None]
    anchor = (wave_z[:, None, None] == 0) & (wave[None, :, None] == 0) & (wave[None, None, :] == 0)

    heat_filter = 1.0 + heat_time * laplace
    laplace_safe = jnp.where(anchor, 1.0, laplace)
    source, heat_filter, laplace_safe, anchor = lax.optimization_barrier(
        (sources.astype(jnp.float32), heat_filter, laplace_safe, anchor)
    )
    spectrum = planes_forward(to_planes(source, cas), cas)
    heat_planes = planes_inverse(spectrum / heat_filter * scale, cas)
    heat = to_pencil(heat_planes, cas, count_x, count_y)

    padded = with_halo(heat, 2)
    divergence = divergence_of_flow(padded, grad_floor)

    div_spectrum = planes_forward(to_planes(divergence, cas), cas)
    potential_spectrum = jnp.where(anchor, 0.0, -div_spectrum / laplace_safe) * scale
    potential = to_pencil(planes_inverse(potential_spectrum, cas), cas, count_x, count_y)
    signs = (2 * labels - 1).astype(jnp.float32)
    return signs * potential


def solution(mesh):
    return jax.shard_map(
        per_device,
        mesh=mesh,
        in_specs=(P("wide", "narrow", None), P("wide", "narrow", None)),
        out_specs=P("wide", "narrow", None),
        check_vma=False,
    )
```

```python
import math

import jax
import jax.numpy as jnp
from jax import lax
from jax.sharding import PartitionSpec as P

highest = lax.Precision.HIGHEST
ALL = ("wide", "narrow")


def cas_table(length):
    positions = jnp.arange(length, dtype=jnp.int32)
    phase_steps = positions[:, None] * positions[None, :] % length
    angles = phase_steps.astype(jnp.float32) * (2.0 * math.pi / length)
    return jnp.cos(angles) + jnp.sin(angles)


def eigen(wavenumber, length):
    angles = wavenumber.astype(jnp.float32) * (2.0 * math.pi / length)
    return 2.0 - 2.0 * jnp.cos(angles)


def to_planes(pencil, cas):
    count_x, count_y, length = pencil.shape
    wide = lax.axis_size("wide")
    narrow = lax.axis_size("narrow")
    span = length // (wide * narrow)
    along_z = jnp.einsum("xyz,zk->kxy", pencil, cas, precision=highest)
    arrived = lax.all_to_all(along_z.reshape(wide * narrow, span, count_x, count_y), ALL, 0, 0)
    arrived = arrived.reshape(wide, narrow, span, count_x, count_y).transpose(2, 0, 3, 1, 4)
    return arrived.reshape(span, wide * count_x, narrow * count_y)


def to_pencil(planes, cas, count_x, count_y, width=0):
    span, length_x, length_y = planes.shape
    wide = lax.axis_size("wide")
    narrow = lax.axis_size("narrow")
    if width:
        planes = windows(planes, 1, count_x, width)
        planes = windows(planes, 3, count_y, width)
    else:
        planes = planes.reshape(span, wide, count_x, narrow, count_y)
    padded_x = count_x + 2 * width
    padded_y = count_y + 2 * width
    send = planes.transpose(1, 3, 0, 2, 4).reshape(wide * narrow, span, padded_x, padded_y)
    arrived = lax.all_to_all(send, ALL, 0, 0)
    spectrum = arrived.reshape(wide * narrow * span, padded_x, padded_y)
    return jnp.einsum("kxy,kz->xyz", spectrum, cas, precision=highest)


def windows(values, axis, count, width):
    length = values.shape[axis]
    blocks = length // count
    padded = jnp.concatenate(
        (
            lax.slice_in_dim(values, length - width, length, axis=axis),
            values,
            lax.slice_in_dim(values, 0, count, axis=axis),
        ),
        axis=axis,
    )
    shape = values.shape[:axis] + (blocks, count) + values.shape[axis + 1 :]
    head = lax.slice_in_dim(padded, 0, length, axis=axis).reshape(shape)
    tail = lax.slice_in_dim(padded, count, count + length, axis=axis).reshape(shape)
    tail = lax.slice_in_dim(tail, 0, 2 * width, axis=axis + 1)
    return jnp.concatenate((head, tail), axis=axis + 1)


def planes_forward(planes, cas):
    along_y = jnp.einsum("kxy,yl->kxl", planes, cas, precision=highest)
    return jnp.einsum("kxl,xm->kml", along_y, cas, precision=highest)


def planes_inverse(spectrum, cas):
    along_x = jnp.einsum("kml,mx->kxl", spectrum, cas, precision=highest)
    return jnp.einsum("kxl,ly->kxy", along_x, cas, precision=highest)


def central_z(values):
    return 0.5 * (jnp.roll(values, -1, 2) - jnp.roll(values, 1, 2))


def divergence_of_flow(heat, grad_floor):
    inner = heat[1:-1, 1:-1]
    grad_x = 0.5 * (heat[2:, 1:-1] - heat[:-2, 1:-1])
    grad_y = 0.5 * (heat[1:-1, 2:] - heat[1:-1, :-2])
    grad_z = central_z(inner)
    magnitude = jnp.sqrt(grad_x * grad_x + grad_y * grad_y + grad_z * grad_z)
    limited = jnp.maximum(magnitude, grad_floor)
    flow_x = -grad_x / limited
    flow_y = -grad_y / limited
    flow_z = -grad_z / limited
    div_x = 0.5 * (flow_x[2:, 1:-1] - flow_x[:-2, 1:-1])
    div_y = 0.5 * (flow_y[1:-1, 2:] - flow_y[1:-1, :-2])
    div_z = central_z(flow_z[1:-1, 1:-1])
    return div_x + div_y + div_z


def per_device(sources, labels):
    count_x, count_y, length = sources.shape
    span = length // lax.axis_size(ALL)
    heat_time = (length / 8.0) ** 2
    grad_floor = 0.04 / heat_time
    scale = 1.0 / float(length) ** 3
    cas = cas_table(length)
    wave = jnp.arange(length, dtype=jnp.int32)
    wave_z = lax.axis_index(ALL) * span + jnp.arange(span, dtype=jnp.int32)
    laplace = (
        eigen(wave, length)[None, :, None] + eigen(wave, length)[None, None, :]
    ) + eigen(wave_z, length)[:, None, None]
    anchor = (wave_z[:, None, None] == 0) & (wave[None, :, None] == 0) & (wave[None, None, :] == 0)

    heat_filter = 1.0 + heat_time * laplace
    laplace_safe = jnp.where(anchor, 1.0, laplace)
    source, heat_filter, laplace_safe, anchor = lax.optimization_barrier(
        (sources.astype(jnp.float32), heat_filter, laplace_safe, anchor)
    )
    spectrum = planes_forward(to_planes(source, cas), cas)
    heat_planes = planes_inverse(spectrum / heat_filter * scale, cas)
    padded = to_pencil(heat_planes, cas, count_x, count_y, 2)
    divergence = divergence_of_flow(padded, grad_floor)

    div_spectrum = planes_forward(to_planes(divergence, cas), cas)
    potential_spectrum = jnp.where(anchor, 0.0, -div_spectrum / laplace_safe) * scale
    potential = to_pencil(planes_inverse(potential_spectrum, cas), cas, count_x, count_y)
    signs = (2 * labels - 1).astype(jnp.float32)
    return signs * potential


def solution(mesh):
    return jax.shard_map(
        per_device,
        mesh=mesh,
        in_specs=(P("wide", "narrow", None), P("wide", "narrow", None)),
        out_specs=P("wide", "narrow", None),
        check_vma=False,
    )
```

```python
import math

import jax
import jax.numpy as jnp
from jax import lax
from jax.sharding import PartitionSpec as P

highest = lax.Precision.HIGHEST
ALL = ("wide", "narrow")


def cas_table(length):
    positions = jnp.arange(length, dtype=jnp.int32)
    phase_steps = positions[:, None] * positions[None, :] % length
    angles = phase_steps.astype(jnp.float32) * (2.0 * math.pi / length)
    return jnp.cos(angles) + jnp.sin(angles)


def eigen(wavenumber, length):
    angles = wavenumber.astype(jnp.float32) * (2.0 * math.pi / length)
    return 2.0 - 2.0 * jnp.cos(angles)


def to_planes(pencil, cas):
    count_x, count_y, length = pencil.shape
    wide = lax.axis_size("wide")
    narrow = lax.axis_size("narrow")
    span = length // (wide * narrow)
    along_z = jnp.einsum("xyz,zk->kxy", pencil, cas, precision=highest)
    arrived = lax.all_to_all(along_z.reshape(wide * narrow, span, count_x, count_y), ALL, 0, 0)
    arrived = arrived.reshape(wide, narrow, span, count_x, count_y).transpose(2, 0, 3, 1, 4)
    return arrived.reshape(span, wide * count_x, narrow * count_y)


def to_pencil(planes, cas, count_x, count_y, width=0):
    span, length_x, length_y = planes.shape
    wide = lax.axis_size("wide")
    narrow = lax.axis_size("narrow")
    if width:
        planes = windows(planes, 1, count_x, width)
        planes = windows(planes, 3, count_y, width)
    else:
        planes = planes.reshape(span, wide, count_x, narrow, count_y)
    padded_x = count_x + 2 * width
    padded_y = count_y + 2 * width
    send = planes.transpose(1, 3, 0, 2, 4).reshape(wide * narrow, span, padded_x, padded_y)
    if width:
        send = send.reshape(wide * narrow, span * padded_x * padded_y)
    arrived = lax.all_to_all(send, ALL, 0, 0)
    spectrum = arrived.reshape(wide * narrow * span, padded_x, padded_y)
    return jnp.einsum("kxy,kz->xyz", spectrum, cas, precision=highest)


def windows(values, axis, count, width):
    length = values.shape[axis]
    blocks = length // count
    padded = jnp.concatenate(
        (
            lax.slice_in_dim(values, length - width, length, axis=axis),
            values,
            lax.slice_in_dim(values, 0, count, axis=axis),
        ),
        axis=axis,
    )
    shape = values.shape[:axis] + (blocks, count) + values.shape[axis + 1 :]
    head = lax.slice_in_dim(padded, 0, length, axis=axis).reshape(shape)
    tail = lax.slice_in_dim(padded, count, count + length, axis=axis).reshape(shape)
    tail = lax.slice_in_dim(tail, 0, 2 * width, axis=axis + 1)
    return jnp.concatenate((head, tail), axis=axis + 1)


def planes_forward(planes, cas):
    along_y = jnp.einsum("kxy,yl->kxl", planes, cas, precision=highest)
    return jnp.einsum("kxl,xm->kml", along_y, cas, precision=highest)


def planes_inverse(spectrum, cas):
    along_x = jnp.einsum("kml,mx->kxl", spectrum, cas, precision=highest)
    return jnp.einsum("kxl,ly->kxy", along_x, cas, precision=highest)


def central_z(values):
    return 0.5 * (jnp.roll(values, -1, 2) - jnp.roll(values, 1, 2))


def divergence_of_flow(heat, grad_floor):
    inner = heat[1:-1, 1:-1]
    grad_x = 0.5 * (heat[2:, 1:-1] - heat[:-2, 1:-1])
    grad_y = 0.5 * (heat[1:-1, 2:] - heat[1:-1, :-2])
    grad_z = central_z(inner)
    magnitude = jnp.sqrt(grad_x * grad_x + grad_y * grad_y + grad_z * grad_z)
    limited = jnp.maximum(magnitude, grad_floor)
    flow_x = -grad_x / limited
    flow_y = -grad_y / limited
    flow_z = -grad_z / limited
    div_x = 0.5 * (flow_x[2:, 1:-1] - flow_x[:-2, 1:-1])
    div_y = 0.5 * (flow_y[1:-1, 2:] - flow_y[1:-1, :-2])
    div_z = central_z(flow_z[1:-1, 1:-1])
    return div_x + div_y + div_z


def per_device(sources, labels):
    count_x, count_y, length = sources.shape
    span = length // lax.axis_size(ALL)
    heat_time = (length / 8.0) ** 2
    grad_floor = 0.04 / heat_time
    scale = 1.0 / float(length) ** 3
    cas = cas_table(length)
    wave = jnp.arange(length, dtype=jnp.int32)
    wave_z = lax.axis_index(ALL) * span + jnp.arange(span, dtype=jnp.int32)
    laplace = (
        eigen(wave, length)[None, :, None] + eigen(wave, length)[None, None, :]
    ) + eigen(wave_z, length)[:, None, None]
    anchor = (wave_z[:, None, None] == 0) & (wave[None, :, None] == 0) & (wave[None, None, :] == 0)

    heat_filter = 1.0 + heat_time * laplace
    laplace_safe = jnp.where(anchor, 1.0, laplace)
    source, heat_filter, laplace_safe, anchor = lax.optimization_barrier(
        (sources.astype(jnp.float32), heat_filter, laplace_safe, anchor)
    )
    spectrum = planes_forward(to_planes(source, cas), cas)
    heat_planes = planes_inverse(spectrum / heat_filter * scale, cas)
    padded = to_pencil(heat_planes, cas, count_x, count_y, 2)
    divergence = divergence_of_flow(padded, grad_floor)

    div_spectrum = planes_forward(to_planes(divergence, cas), cas)
    potential_spectrum = jnp.where(anchor, 0.0, -div_spectrum / laplace_safe) * scale
    potential = to_pencil(planes_inverse(potential_spectrum, cas), cas, count_x, count_y)
    signs = (2 * labels - 1).astype(jnp.float32)
    return signs * potential


def solution(mesh):
    return jax.shard_map(
        per_device,
        mesh=mesh,
        in_specs=(P("wide", "narrow", None), P("wide", "narrow", None)),
        out_specs=P("wide", "narrow", None),
        check_vma=False,
    )
```

```python
import math

import jax
import jax.numpy as jnp
from jax import lax
from jax.sharding import PartitionSpec as P

matmul_precision = lax.Precision.HIGH
ALL = ("wide", "narrow")


def cas_table(length):
    positions = jnp.arange(length, dtype=jnp.int32)
    phase_steps = positions[:, None] * positions[None, :] % length
    angles = phase_steps.astype(jnp.float32) * (2.0 * math.pi / length)
    return jnp.cos(angles) + jnp.sin(angles)


def eigen(wavenumber, length):
    angles = wavenumber.astype(jnp.float32) * (2.0 * math.pi / length)
    return 2.0 - 2.0 * jnp.cos(angles)


def to_planes(pencil, cas):
    count_x, count_y, length = pencil.shape
    wide = lax.axis_size("wide")
    narrow = lax.axis_size("narrow")
    span = length // (wide * narrow)
    along_z = jnp.einsum("xyz,zk->kxy", pencil, cas, precision=matmul_precision)
    arrived = lax.all_to_all(along_z.reshape(wide * narrow, span, count_x, count_y), ALL, 0, 0)
    arrived = arrived.reshape(wide, narrow, span, count_x, count_y).transpose(2, 0, 3, 1, 4)
    return arrived.reshape(span, wide * count_x, narrow * count_y)


def to_pencil(planes, cas, count_x, count_y, width=0):
    span, length_x, length_y = planes.shape
    wide = lax.axis_size("wide")
    narrow = lax.axis_size("narrow")
    if width:
        planes = windows(planes, 1, count_x, width)
        planes = windows(planes, 3, count_y, width)
    else:
        planes = planes.reshape(span, wide, count_x, narrow, count_y)
    padded_x = count_x + 2 * width
    padded_y = count_y + 2 * width
    send = planes.transpose(1, 3, 0, 2, 4).reshape(wide * narrow, span, padded_x, padded_y)
    if width:
        send = send.reshape(wide * narrow, span * padded_x * padded_y)
    arrived = lax.all_to_all(send, ALL, 0, 0)
    spectrum = arrived.reshape(wide * narrow * span, padded_x, padded_y)
    return jnp.einsum("kxy,kz->xyz", spectrum, cas, precision=matmul_precision)


def windows(values, axis, count, width):
    length = values.shape[axis]
    blocks = length // count
    padded = jnp.concatenate(
        (
            lax.slice_in_dim(values, length - width, length, axis=axis),
            values,
            lax.slice_in_dim(values, 0, count, axis=axis),
        ),
        axis=axis,
    )
    shape = values.shape[:axis] + (blocks, count) + values.shape[axis + 1 :]
    head = lax.slice_in_dim(padded, 0, length, axis=axis).reshape(shape)
    tail = lax.slice_in_dim(padded, count, count + length, axis=axis).reshape(shape)
    tail = lax.slice_in_dim(tail, 0, 2 * width, axis=axis + 1)
    return jnp.concatenate((head, tail), axis=axis + 1)


def planes_forward(planes, cas):
    along_y = jnp.einsum("kxy,yl->kxl", planes, cas, precision=matmul_precision)
    return jnp.einsum("kxl,xm->kml", along_y, cas, precision=matmul_precision)


def planes_inverse(spectrum, cas):
    along_x = jnp.einsum("kml,mx->kxl", spectrum, cas, precision=matmul_precision)
    return jnp.einsum("kxl,ly->kxy", along_x, cas, precision=matmul_precision)


def central_z(values):
    return 0.5 * (jnp.roll(values, -1, 2) - jnp.roll(values, 1, 2))


def divergence_of_flow(heat, grad_floor):
    inner = heat[1:-1, 1:-1]
    grad_x = 0.5 * (heat[2:, 1:-1] - heat[:-2, 1:-1])
    grad_y = 0.5 * (heat[1:-1, 2:] - heat[1:-1, :-2])
    grad_z = central_z(inner)
    magnitude = jnp.sqrt(grad_x * grad_x + grad_y * grad_y + grad_z * grad_z)
    limited = jnp.maximum(magnitude, grad_floor)
    flow_x = -grad_x / limited
    flow_y = -grad_y / limited
    flow_z = -grad_z / limited
    div_x = 0.5 * (flow_x[2:, 1:-1] - flow_x[:-2, 1:-1])
    div_y = 0.5 * (flow_y[1:-1, 2:] - flow_y[1:-1, :-2])
    div_z = central_z(flow_z[1:-1, 1:-1])
    return div_x + div_y + div_z


def per_device(sources, labels):
    count_x, count_y, length = sources.shape
    span = length // lax.axis_size(ALL)
    heat_time = (length / 8.0) ** 2
    grad_floor = 0.04 / heat_time
    scale = 1.0 / float(length) ** 3
    cas = cas_table(length)
    wave = jnp.arange(length, dtype=jnp.int32)
    wave_z = lax.axis_index(ALL) * span + jnp.arange(span, dtype=jnp.int32)
    laplace = (
        eigen(wave, length)[None, :, None] + eigen(wave, length)[None, None, :]
    ) + eigen(wave_z, length)[:, None, None]
    anchor = (wave_z[:, None, None] == 0) & (wave[None, :, None] == 0) & (wave[None, None, :] == 0)

    heat_filter = 1.0 + heat_time * laplace
    laplace_safe = jnp.where(anchor, 1.0, laplace)
    source, heat_filter, laplace_safe, anchor = lax.optimization_barrier(
        (sources.astype(jnp.float32), heat_filter, laplace_safe, anchor)
    )
    spectrum = planes_forward(to_planes(source, cas), cas)
    heat_planes = planes_inverse(spectrum / heat_filter * scale, cas)
    padded = to_pencil(heat_planes, cas, count_x, count_y, 2)
    divergence = divergence_of_flow(padded, grad_floor)

    div_spectrum = planes_forward(to_planes(divergence, cas), cas)
    potential_spectrum = jnp.where(anchor, 0.0, -div_spectrum / laplace_safe) * scale
    potential = to_pencil(planes_inverse(potential_spectrum, cas), cas, count_x, count_y)
    signs = (2 * labels - 1).astype(jnp.float32)
    return signs * potential


def solution(mesh):
    return jax.shard_map(
        per_device,
        mesh=mesh,
        in_specs=(P("wide", "narrow", None), P("wide", "narrow", None)),
        out_specs=P("wide", "narrow", None),
        check_vma=False,
    )
```

```python
import math

import jax
import jax.numpy as jnp
from jax import lax
from jax.sharding import PartitionSpec as P

matmul_precision = lax.Precision.HIGH
ALL = ("wide", "narrow")


def cas_table(length):
    positions = jnp.arange(length, dtype=jnp.int32)
    phase_steps = positions[:, None] * positions[None, :] % length
    angles = phase_steps.astype(jnp.float32) * (2.0 * math.pi / length)
    return jnp.cos(angles) + jnp.sin(angles)


def cas_columns(length, positions):
    wavenumbers = jnp.arange(length, dtype=jnp.int32).reshape((length,) + (1,) * positions.ndim)
    phase_steps = wavenumbers * positions[None] % length
    angles = phase_steps.astype(jnp.float32) * (2.0 * math.pi / length)
    return jnp.cos(angles) + jnp.sin(angles)


def window_positions(length, count, width):
    blocks = length // count
    starts = jnp.arange(blocks, dtype=jnp.int32)[:, None] * count - width
    return (starts + jnp.arange(count + 2 * width, dtype=jnp.int32)[None, :]) % length


def eigen(wavenumber, length):
    angles = wavenumber.astype(jnp.float32) * (2.0 * math.pi / length)
    return 2.0 - 2.0 * jnp.cos(angles)


def to_planes(pencil, cas):
    count_x, count_y, length = pencil.shape
    wide = lax.axis_size("wide")
    narrow = lax.axis_size("narrow")
    span = length // (wide * narrow)
    along_z = jnp.einsum("xyz,zk->kxy", pencil, cas, precision=matmul_precision)
    arrived = lax.all_to_all(along_z.reshape(wide * narrow, span, count_x, count_y), ALL, 0, 0)
    arrived = arrived.reshape(wide, narrow, span, count_x, count_y).transpose(2, 0, 3, 1, 4)
    return arrived.reshape(span, wide * count_x, narrow * count_y)


def to_pencil(planes, cas, count_x, count_y):
    span, _, _ = planes.shape
    wide = lax.axis_size("wide")
    narrow = lax.axis_size("narrow")
    send = planes.reshape(span, wide, count_x, narrow, count_y).transpose(1, 3, 0, 2, 4)
    arrived = lax.all_to_all(send.reshape(wide * narrow, span, count_x, count_y), ALL, 0, 0)
    spectrum = arrived.reshape(wide * narrow * span, count_x, count_y)
    return jnp.einsum("kxy,kz->xyz", spectrum, cas, precision=matmul_precision)


def to_pencil_with_halo(spectrum, cas, cas_x, cas_y):
    span, length, _ = spectrum.shape
    _, wide, padded_x = cas_x.shape
    _, narrow, padded_y = cas_y.shape
    along_x = jnp.einsum("kml,mwi->kwil", spectrum, cas_x, precision=matmul_precision)
    windows = jnp.einsum("kwil,lqj->wqkij", along_x, cas_y, precision=matmul_precision)
    send = windows.reshape(wide * narrow, span * padded_x * padded_y)
    arrived = lax.all_to_all(send, ALL, 0, 0)
    spectrum_z = arrived.reshape(wide * narrow * span, padded_x * padded_y)
    values = jnp.einsum("kr,kz->rz", spectrum_z, cas, precision=matmul_precision)
    return values.reshape(padded_x, padded_y, length)


def planes_forward(planes, cas):
    along_y = jnp.einsum("kxy,yl->kxl", planes, cas, precision=matmul_precision)
    return jnp.einsum("kxl,xm->kml", along_y, cas, precision=matmul_precision)


def planes_inverse(spectrum, cas):
    along_x = jnp.einsum("kml,mx->kxl", spectrum, cas, precision=matmul_precision)
    return jnp.einsum("kxl,ly->kxy", along_x, cas, precision=matmul_precision)


def central_z(values):
    return 0.5 * (jnp.roll(values, -1, 2) - jnp.roll(values, 1, 2))


def divergence_of_flow(heat, grad_floor):
    inner = heat[1:-1, 1:-1]
    grad_x = 0.5 * (heat[2:, 1:-1] - heat[:-2, 1:-1])
    grad_y = 0.5 * (heat[1:-1, 2:] - heat[1:-1, :-2])
    grad_z = central_z(inner)
    magnitude = jnp.sqrt(grad_x * grad_x + grad_y * grad_y + grad_z * grad_z)
    limited = jnp.maximum(magnitude, grad_floor)
    flow_x = -grad_x / limited
    flow_y = -grad_y / limited
    flow_z = -grad_z / limited
    div_x = 0.5 * (flow_x[2:, 1:-1] - flow_x[:-2, 1:-1])
    div_y = 0.5 * (flow_y[1:-1, 2:] - flow_y[1:-1, :-2])
    div_z = central_z(flow_z[1:-1, 1:-1])
    return div_x + div_y + div_z


def per_device(sources, labels):
    count_x, count_y, length = sources.shape
    span = length // lax.axis_size(ALL)
    heat_time = (length / 8.0) ** 2
    grad_floor = 0.04 / heat_time
    scale = 1.0 / float(length) ** 3
    cas = cas_table(length)
    wave = jnp.arange(length, dtype=jnp.int32)
    wave_z = lax.axis_index(ALL) * span + jnp.arange(span, dtype=jnp.int32)
    laplace = (
        eigen(wave, length)[None, :, None] + eigen(wave, length)[None, None, :]
    ) + eigen(wave_z, length)[:, None, None]
    anchor = (wave_z[:, None, None] == 0) & (wave[None, :, None] == 0) & (wave[None, None, :] == 0)

    heat_filter = 1.0 + heat_time * laplace
    laplace_safe = jnp.where(anchor, 1.0, laplace)
    cas_x = cas_columns(length, window_positions(length, count_x, 2))
    cas_y = cas_columns(length, window_positions(length, count_y, 4))
    source, heat_filter, laplace_safe, anchor, cas_x, cas_y = lax.optimization_barrier(
        (sources.astype(jnp.float32), heat_filter, laplace_safe, anchor, cas_x, cas_y)
    )
    spectrum = planes_forward(to_planes(source, cas), cas)
    padded = to_pencil_with_halo(spectrum / heat_filter * scale, cas, cas_x, cas_y)
    divergence = divergence_of_flow(padded[:, 2:-2], grad_floor)

    div_spectrum = planes_forward(to_planes(divergence, cas), cas)
    potential_spectrum = jnp.where(anchor, 0.0, -div_spectrum / laplace_safe) * scale
    potential = to_pencil(planes_inverse(potential_spectrum, cas), cas, count_x, count_y)
    signs = (2 * labels - 1).astype(jnp.float32)
    return signs * potential


def solution(mesh):
    return jax.shard_map(
        per_device,
        mesh=mesh,
        in_specs=(P("wide", "narrow", None), P("wide", "narrow", None)),
        out_specs=P("wide", "narrow", None),
        check_vma=False,
    )
```

```python
import math

import jax
import jax.numpy as jnp
from jax import lax
from jax.sharding import PartitionSpec as P

matmul_precision = lax.Precision.HIGH
ALL = ("wide", "narrow")


def cas_table(length):
    positions = jnp.arange(length, dtype=jnp.int32)
    phase_steps = positions[:, None] * positions[None, :] % length
    angles = phase_steps.astype(jnp.float32) * (2.0 * math.pi / length)
    return jnp.cos(angles) + jnp.sin(angles)


def cas_columns(length, positions):
    wavenumbers = jnp.arange(length, dtype=jnp.int32).reshape((length,) + (1,) * positions.ndim)
    phase_steps = wavenumbers * positions[None] % length
    angles = phase_steps.astype(jnp.float32) * (2.0 * math.pi / length)
    return jnp.cos(angles) + jnp.sin(angles)


def window_positions(length, count, width):
    blocks = length // count
    starts = jnp.arange(blocks, dtype=jnp.int32)[:, None] * count - width
    return (starts + jnp.arange(count + 2 * width, dtype=jnp.int32)[None, :]) % length


def eigen(wavenumber, length):
    angles = wavenumber.astype(jnp.float32) * (2.0 * math.pi / length)
    return 2.0 - 2.0 * jnp.cos(angles)


def to_planes(pencil, cas):
    count_x, count_y, length = pencil.shape
    wide = lax.axis_size("wide")
    narrow = lax.axis_size("narrow")
    span = length // (wide * narrow)
    along_z = jnp.einsum("xyz,zk->kxy", pencil, cas, precision=matmul_precision)
    arrived = lax.all_to_all(along_z.reshape(wide * narrow, span, count_x, count_y), ALL, 0, 0)
    arrived = arrived.reshape(wide, narrow, span, count_x, count_y).transpose(2, 0, 3, 1, 4)
    return arrived.reshape(span, wide * count_x, narrow * count_y)


def to_pencil(planes, cas, count_x, count_y):
    span, _, _ = planes.shape
    wide = lax.axis_size("wide")
    narrow = lax.axis_size("narrow")
    send = planes.reshape(span, wide, count_x, narrow, count_y).transpose(1, 3, 0, 2, 4)
    arrived = lax.all_to_all(send.reshape(wide * narrow, span, count_x, count_y), ALL, 0, 0)
    spectrum = arrived.reshape(wide * narrow * span, count_x, count_y)
    return jnp.einsum("kxy,kz->xyz", spectrum, cas, precision=matmul_precision)


def to_pencil_with_halo(spectrum, cas, cas_x, cas_y):
    span, length, _ = spectrum.shape
    _, wide, padded_x = cas_x.shape
    _, narrow, padded_y = cas_y.shape
    along_x = jnp.einsum("kml,mwi->kwil", spectrum, cas_x, precision=matmul_precision)
    windows = jnp.einsum("kwil,lqj->wqkij", along_x, cas_y, precision=matmul_precision)
    send = windows.reshape(wide * narrow, span * padded_x * padded_y)
    arrived = lax.all_to_all(send, ALL, 0, 0)
    spectrum_z = arrived.reshape(wide * narrow * span, padded_x * padded_y)
    values = jnp.einsum("kr,kz->rz", spectrum_z, cas, precision=matmul_precision)
    return values.reshape(padded_x, padded_y, length)


def planes_forward(planes, cas):
    along_y = jnp.einsum("kxy,yl->kxl", planes, cas, precision=matmul_precision)
    return jnp.einsum("kxl,xm->kml", along_y, cas, precision=matmul_precision)


def planes_inverse(spectrum, cas):
    along_x = jnp.einsum("kml,mx->kxl", spectrum, cas, precision=matmul_precision)
    return jnp.einsum("kxl,ly->kxy", along_x, cas, precision=matmul_precision)


def central_z(values):
    return 0.5 * (jnp.roll(values, -1, 2) - jnp.roll(values, 1, 2))


def divergence_of_flow(heat, grad_floor):
    inner = heat[1:-1, 1:-1]
    grad_x = 0.5 * (heat[2:, 1:-1] - heat[:-2, 1:-1])
    grad_y = 0.5 * (heat[1:-1, 2:] - heat[1:-1, :-2])
    grad_z = central_z(inner)
    magnitude = jnp.sqrt(grad_x * grad_x + grad_y * grad_y + grad_z * grad_z)
    limited = jnp.maximum(magnitude, grad_floor)
    flow_x = -grad_x / limited
    flow_y = -grad_y / limited
    flow_z = -grad_z / limited
    div_x = 0.5 * (flow_x[2:, 1:-1] - flow_x[:-2, 1:-1])
    div_y = 0.5 * (flow_y[1:-1, 2:] - flow_y[1:-1, :-2])
    div_z = central_z(flow_z[1:-1, 1:-1])
    return div_x + div_y + div_z


def per_device(sources, labels):
    count_x, count_y, length = sources.shape
    span = length // lax.axis_size(ALL)
    heat_time = (length / 8.0) ** 2
    grad_floor = 0.04 / heat_time
    scale = 1.0 / float(length) ** 3
    cas = cas_table(length)
    wave = jnp.arange(length, dtype=jnp.int32)
    wave_z = lax.axis_index(ALL) * span + jnp.arange(span, dtype=jnp.int32)
    laplace = (
        eigen(wave, length)[None, :, None] + eigen(wave, length)[None, None, :]
    ) + eigen(wave_z, length)[:, None, None]
    anchor = (wave_z[:, None, None] == 0) & (wave[None, :, None] == 0) & (wave[None, None, :] == 0)

    heat_filter = 1.0 + heat_time * laplace
    laplace_safe = jnp.where(anchor, 1.0, laplace)
    cas_x = cas_columns(length, window_positions(length, count_x, 2))
    cas_y = cas_columns(length, window_positions(length, count_y, 4))
    source = sources.astype(jnp.float32)
    spectrum = planes_forward(to_planes(source, cas), cas)
    padded = to_pencil_with_halo(spectrum / heat_filter * scale, cas, cas_x, cas_y)
    divergence = divergence_of_flow(padded[:, 2:-2], grad_floor)

    div_spectrum = planes_forward(to_planes(divergence, cas), cas)
    potential_spectrum = jnp.where(anchor, 0.0, -div_spectrum / laplace_safe) * scale
    potential = to_pencil(planes_inverse(potential_spectrum, cas), cas, count_x, count_y)
    signs = (2 * labels - 1).astype(jnp.float32)
    return signs * potential


def solution(mesh):
    return jax.shard_map(
        per_device,
        mesh=mesh,
        in_specs=(P("wide", "narrow", None), P("wide", "narrow", None)),
        out_specs=P("wide", "narrow", None),
        check_vma=False,
    )
```

```python
import math

import jax
import jax.numpy as jnp
from jax import lax
from jax.sharding import PartitionSpec as P

matmul_precision = lax.Precision.HIGH
ALL = ("wide", "narrow")


def cas_table(length):
    positions = jnp.arange(length, dtype=jnp.int32)
    phase_steps = positions[:, None] * positions[None, :] % length
    angles = phase_steps.astype(jnp.float32) * (2.0 * math.pi / length)
    return jnp.cos(angles) + jnp.sin(angles)


def cas_columns(length, positions):
    wavenumbers = jnp.arange(length, dtype=jnp.int32).reshape((length,) + (1,) * positions.ndim)
    phase_steps = wavenumbers * positions[None] % length
    angles = phase_steps.astype(jnp.float32) * (2.0 * math.pi / length)
    return jnp.cos(angles) + jnp.sin(angles)


def window_positions(length, count, width):
    blocks = length // count
    starts = jnp.arange(blocks, dtype=jnp.int32)[:, None] * count - width
    return (starts + jnp.arange(count + 2 * width, dtype=jnp.int32)[None, :]) % length


def eigen(wavenumber, length):
    angles = wavenumber.astype(jnp.float32) * (2.0 * math.pi / length)
    return 2.0 - 2.0 * jnp.cos(angles)


def to_planes(pencil, cas):
    count_x, count_y, length = pencil.shape
    wide = lax.axis_size("wide")
    narrow = lax.axis_size("narrow")
    span = length // (wide * narrow)
    along_z = jnp.einsum("xyz,zk->kxy", pencil, cas, precision=matmul_precision)
    arrived = lax.all_to_all(along_z.reshape(wide * narrow, span, count_x, count_y), ALL, 0, 0)
    arrived = arrived.reshape(wide, narrow, span, count_x, count_y).transpose(2, 0, 3, 1, 4)
    return arrived.reshape(span, wide * count_x, narrow * count_y)


def to_pencil(planes, cas, count_x, count_y):
    span, _, _ = planes.shape
    wide = lax.axis_size("wide")
    narrow = lax.axis_size("narrow")
    send = planes.reshape(span, wide, count_x, narrow, count_y).transpose(1, 3, 0, 2, 4)
    arrived = lax.all_to_all(send.reshape(wide * narrow, span, count_x, count_y), ALL, 0, 0)
    spectrum = arrived.reshape(wide * narrow * span, count_x, count_y)
    return jnp.einsum("kxy,kz->xyz", spectrum, cas, precision=matmul_precision)


def to_pencil_with_halo(spectrum, cas, cas_x, cas_y):
    span, length, _ = spectrum.shape
    _, wide, padded_x = cas_x.shape
    _, narrow, padded_y = cas_y.shape
    along_x = jnp.einsum("kml,mwi->kwil", spectrum, cas_x, precision=matmul_precision)
    windows = jnp.einsum("kwil,lqj->wqkij", along_x, cas_y, precision=matmul_precision)
    send = windows.reshape(wide * narrow, span * padded_x * padded_y)
    arrived = lax.all_to_all(send, ALL, 0, 0)
    spectrum_z = arrived.reshape(wide * narrow * span, padded_x * padded_y)
    values = jnp.einsum("kr,kz->rz", spectrum_z, cas, precision=matmul_precision)
    return values.reshape(padded_x, padded_y, length)


def planes_forward(planes, cas):
    along_y = jnp.einsum("kxy,yl->kxl", planes, cas, precision=matmul_precision)
    return jnp.einsum("kxl,xm->kml", along_y, cas, precision=matmul_precision)


def planes_inverse(spectrum, cas):
    along_x = jnp.einsum("kml,mx->kxl", spectrum, cas, precision=matmul_precision)
    return jnp.einsum("kxl,ly->kxy", along_x, cas, precision=matmul_precision)


def central_z(values):
    return 0.5 * (jnp.roll(values, -1, 2) - jnp.roll(values, 1, 2))


def divergence_of_flow(heat, grad_floor):
    inner = heat[1:-1, 1:-1]
    grad_x = 0.5 * (heat[2:, 1:-1] - heat[:-2, 1:-1])
    grad_y = 0.5 * (heat[1:-1, 2:] - heat[1:-1, :-2])
    grad_z = central_z(inner)
    magnitude = jnp.sqrt(grad_x * grad_x + grad_y * grad_y + grad_z * grad_z)
    limited = jnp.maximum(magnitude, grad_floor)
    flow_x = -grad_x / limited
    flow_y = -grad_y / limited
    flow_z = -grad_z / limited
    div_x = 0.5 * (flow_x[2:, 1:-1] - flow_x[:-2, 1:-1])
    div_y = 0.5 * (flow_y[1:-1, 2:] - flow_y[1:-1, :-2])
    div_z = central_z(flow_z[1:-1, 1:-1])
    return div_x + div_y + div_z


def per_device(sources, labels):
    count_x, count_y, length = sources.shape
    span = length // lax.axis_size(ALL)
    heat_time = (length / 8.0) ** 2
    grad_floor = 0.04 / heat_time
    scale = 1.0 / float(length) ** 3
    cas = cas_table(length)
    wave = jnp.arange(length, dtype=jnp.int32)
    wave_z = lax.axis_index(ALL) * span + jnp.arange(span, dtype=jnp.int32)
    laplace = (
        eigen(wave, length)[None, :, None] + eigen(wave, length)[None, None, :]
    ) + eigen(wave_z, length)[:, None, None]
    anchor = (wave_z[:, None, None] == 0) & (wave[None, :, None] == 0) & (wave[None, None, :] == 0)

    heat_filter = 1.0 + heat_time * laplace
    laplace_safe = jnp.where(anchor, 1.0, laplace)
    cas_x, cas_y = lax.optimization_barrier(
        (
            cas_columns(length, window_positions(length, count_x, 2)),
            cas_columns(length, window_positions(length, count_y, 4)),
        )
    )
    source = sources.astype(jnp.float32)
    spectrum = planes_forward(to_planes(source, cas), cas)
    padded = to_pencil_with_halo(spectrum / heat_filter * scale, cas, cas_x, cas_y)
    divergence = divergence_of_flow(padded[:, 2:-2], grad_floor)

    div_spectrum = planes_forward(to_planes(divergence, cas), cas)
    potential_spectrum = jnp.where(anchor, 0.0, -div_spectrum / laplace_safe) * scale
    potential = to_pencil(planes_inverse(potential_spectrum, cas), cas, count_x, count_y)
    signs = (2 * labels - 1).astype(jnp.float32)
    return signs * potential


def solution(mesh):
    return jax.shard_map(
        per_device,
        mesh=mesh,
        in_specs=(P("wide", "narrow", None), P("wide", "narrow", None)),
        out_specs=P("wide", "narrow", None),
        check_vma=False,
    )
```

```python
import math

import jax
import jax.numpy as jnp
from jax import lax
from jax.sharding import PartitionSpec as P

matmul_precision = lax.Precision.HIGH
ALL = ("wide", "narrow")


def cas_table(length):
    positions = jnp.arange(length, dtype=jnp.int32)
    phase_steps = positions[:, None] * positions[None, :] % length
    angles = phase_steps.astype(jnp.float32) * (2.0 * math.pi / length)
    return jnp.cos(angles) + jnp.sin(angles)


def cas_columns(length, positions):
    wavenumbers = jnp.arange(length, dtype=jnp.int32).reshape((length,) + (1,) * positions.ndim)
    phase_steps = wavenumbers * positions[None] % length
    angles = phase_steps.astype(jnp.float32) * (2.0 * math.pi / length)
    return jnp.cos(angles) + jnp.sin(angles)


def window_positions(length, count, width):
    blocks = length // count
    starts = jnp.arange(blocks, dtype=jnp.int32)[:, None] * count - width
    return (starts + jnp.arange(count + 2 * width, dtype=jnp.int32)[None, :]) % length


def eigen(wavenumber, length):
    angles = wavenumber.astype(jnp.float32) * (2.0 * math.pi / length)
    return 2.0 - 2.0 * jnp.cos(angles)


def to_planes(pencil, cas):
    count_x, count_y, length = pencil.shape
    wide = lax.axis_size("wide")
    narrow = lax.axis_size("narrow")
    span = length // (wide * narrow)
    along_z = jnp.einsum("xyz,zk->kxy", pencil, cas, precision=matmul_precision)
    arrived = lax.all_to_all(along_z.reshape(wide * narrow, span, count_x, count_y), ALL, 0, 0)
    arrived = arrived.reshape(wide, narrow, span, count_x, count_y)
    along_y = jnp.einsum(
        "wqkxy,qyl->kwxl", arrived, cas.reshape(narrow, count_y, length), precision=matmul_precision
    )
    return along_y.reshape(span, wide * count_x, length)


def to_pencil(planes, cas, count_x, count_y):
    span, _, _ = planes.shape
    wide = lax.axis_size("wide")
    narrow = lax.axis_size("narrow")
    send = planes.reshape(span, wide, count_x, narrow, count_y).transpose(1, 3, 0, 2, 4)
    arrived = lax.all_to_all(send.reshape(wide * narrow, span, count_x, count_y), ALL, 0, 0)
    spectrum = arrived.reshape(wide * narrow * span, count_x, count_y)
    return jnp.einsum("kxy,kz->xyz", spectrum, cas, precision=matmul_precision)


def to_pencil_with_halo(spectrum, cas, cas_x, cas_y):
    span, length, _ = spectrum.shape
    _, wide, padded_x = cas_x.shape
    _, narrow, padded_y = cas_y.shape
    along_x = jnp.einsum("kml,mwi->kwil", spectrum, cas_x, precision=matmul_precision)
    windows = jnp.einsum("kwil,lqj->wqkij", along_x, cas_y, precision=matmul_precision)
    send = windows.reshape(wide * narrow, span * padded_x * padded_y)
    arrived = lax.all_to_all(send, ALL, 0, 0)
    spectrum_z = arrived.reshape(wide * narrow * span, padded_x * padded_y)
    values = jnp.einsum("kr,kz->rz", spectrum_z, cas, precision=matmul_precision)
    return values.reshape(padded_x, padded_y, length)


def planes_forward(along_y, cas):
    return jnp.einsum("kxl,xm->kml", along_y, cas, precision=matmul_precision)


def planes_inverse(spectrum, cas):
    along_x = jnp.einsum("kml,mx->kxl", spectrum, cas, precision=matmul_precision)
    return jnp.einsum("kxl,ly->kxy", along_x, cas, precision=matmul_precision)


def central_z(values):
    return 0.5 * (jnp.roll(values, -1, 2) - jnp.roll(values, 1, 2))


def divergence_of_flow(heat, grad_floor):
    inner = heat[1:-1, 1:-1]
    grad_x = 0.5 * (heat[2:, 1:-1] - heat[:-2, 1:-1])
    grad_y = 0.5 * (heat[1:-1, 2:] - heat[1:-1, :-2])
    grad_z = central_z(inner)
    magnitude = jnp.sqrt(grad_x * grad_x + grad_y * grad_y + grad_z * grad_z)
    limited = jnp.maximum(magnitude, grad_floor)
    flow_x = -grad_x / limited
    flow_y = -grad_y / limited
    flow_z = -grad_z / limited
    div_x = 0.5 * (flow_x[2:, 1:-1] - flow_x[:-2, 1:-1])
    div_y = 0.5 * (flow_y[1:-1, 2:] - flow_y[1:-1, :-2])
    div_z = central_z(flow_z[1:-1, 1:-1])
    return div_x + div_y + div_z


def per_device(sources, labels):
    count_x, count_y, length = sources.shape
    span = length // lax.axis_size(ALL)
    heat_time = (length / 8.0) ** 2
    grad_floor = 0.04 / heat_time
    scale = 1.0 / float(length) ** 3
    cas = cas_table(length)
    wave = jnp.arange(length, dtype=jnp.int32)
    wave_z = lax.axis_index(ALL) * span + jnp.arange(span, dtype=jnp.int32)
    laplace = (
        eigen(wave, length)[None, :, None] + eigen(wave, length)[None, None, :]
    ) + eigen(wave_z, length)[:, None, None]
    anchor = (wave_z[:, None, None] == 0) & (wave[None, :, None] == 0) & (wave[None, None, :] == 0)

    heat_filter = 1.0 + heat_time * laplace
    laplace_safe = jnp.where(anchor, 1.0, laplace)
    cas_x, cas_y = lax.optimization_barrier(
        (
            cas_columns(length, window_positions(length, count_x, 2)),
            cas_columns(length, window_positions(length, count_y, 4)),
        )
    )
    source = sources.astype(jnp.float32)
    spectrum = planes_forward(to_planes(source, cas), cas)
    padded = to_pencil_with_halo(spectrum / heat_filter * scale, cas, cas_x, cas_y)
    divergence = divergence_of_flow(padded[:, 2:-2], grad_floor)

    div_spectrum = planes_forward(to_planes(divergence, cas), cas)
    potential_spectrum = jnp.where(anchor, 0.0, -div_spectrum / laplace_safe) * scale
    potential = to_pencil(planes_inverse(potential_spectrum, cas), cas, count_x, count_y)
    signs = (2 * labels - 1).astype(jnp.float32)
    return signs * potential


def solution(mesh):
    return jax.shard_map(
        per_device,
        mesh=mesh,
        in_specs=(P("wide", "narrow", None), P("wide", "narrow", None)),
        out_specs=P("wide", "narrow", None),
        check_vma=False,
    )
```

```python
import math

import jax
import jax.numpy as jnp
from jax import lax
from jax.sharding import PartitionSpec as P

matmul_precision = lax.Precision.HIGH
ALL = ("wide", "narrow")


def cas_table(length):
    positions = jnp.arange(length, dtype=jnp.int32)
    phase_steps = positions[:, None] * positions[None, :] % length
    angles = phase_steps.astype(jnp.float32) * (2.0 * math.pi / length)
    return jnp.cos(angles) + jnp.sin(angles)


def cas_columns(length, positions):
    wavenumbers = jnp.arange(length, dtype=jnp.int32).reshape((length,) + (1,) * positions.ndim)
    phase_steps = wavenumbers * positions[None] % length
    angles = phase_steps.astype(jnp.float32) * (2.0 * math.pi / length)
    return jnp.cos(angles) + jnp.sin(angles)


def window_positions(length, count, width):
    blocks = length // count
    starts = jnp.arange(blocks, dtype=jnp.int32)[:, None] * count - width
    return (starts + jnp.arange(count + 2 * width, dtype=jnp.int32)[None, :]) % length


def eigen(wavenumber, length):
    angles = wavenumber.astype(jnp.float32) * (2.0 * math.pi / length)
    return 2.0 - 2.0 * jnp.cos(angles)


def to_planes(pencil, cas):
    count_x, count_y, length = pencil.shape
    wide = lax.axis_size("wide")
    narrow = lax.axis_size("narrow")
    span = length // (wide * narrow)
    along_z = jnp.einsum("xyz,zk->kxy", pencil, cas, precision=matmul_precision)
    arrived = lax.all_to_all(along_z.reshape(wide * narrow, span, count_x, count_y), ALL, 0, 0)
    arrived = arrived.reshape(wide, narrow, span, count_x, count_y)
    along_y = jnp.einsum(
        "wqkxy,qyl->kwxl", arrived, cas.reshape(narrow, count_y, length), precision=matmul_precision
    )
    return along_y.reshape(span, wide * count_x, length)


def to_pencil(spectrum, cas, count_x, count_y):
    span, length, _ = spectrum.shape
    wide = lax.axis_size("wide")
    narrow = lax.axis_size("narrow")
    along_x = jnp.einsum("kml,mx->kxl", spectrum, cas, precision=matmul_precision)
    send = jnp.einsum(
        "kwxl,lqy->wqkxy",
        along_x.reshape(span, wide, count_x, length),
        cas.reshape(length, narrow, count_y),
        precision=matmul_precision,
    )
    arrived = lax.all_to_all(send.reshape(wide * narrow, span, count_x, count_y), ALL, 0, 0)
    spectrum_z = arrived.reshape(wide * narrow * span, count_x, count_y)
    return jnp.einsum("kxy,kz->xyz", spectrum_z, cas, precision=matmul_precision)


def to_pencil_with_halo(spectrum, cas, cas_x, cas_y):
    span, length, _ = spectrum.shape
    _, wide, padded_x = cas_x.shape
    _, narrow, padded_y = cas_y.shape
    along_x = jnp.einsum("kml,mwi->kwil", spectrum, cas_x, precision=matmul_precision)
    windows = jnp.einsum("kwil,lqj->wqkij", along_x, cas_y, precision=matmul_precision)
    send = windows.reshape(wide * narrow, span * padded_x * padded_y)
    arrived = lax.all_to_all(send, ALL, 0, 0)
    spectrum_z = arrived.reshape(wide * narrow * span, padded_x * padded_y)
    values = jnp.einsum("kr,kz->rz", spectrum_z, cas, precision=matmul_precision)
    return values.reshape(padded_x, padded_y, length)


def planes_forward(along_y, cas):
    return jnp.einsum("kxl,xm->kml", along_y, cas, precision=matmul_precision)


def central_z(values):
    return 0.5 * (jnp.roll(values, -1, 2) - jnp.roll(values, 1, 2))


def divergence_of_flow(heat, grad_floor):
    inner = heat[1:-1, 1:-1]
    grad_x = 0.5 * (heat[2:, 1:-1] - heat[:-2, 1:-1])
    grad_y = 0.5 * (heat[1:-1, 2:] - heat[1:-1, :-2])
    grad_z = central_z(inner)
    magnitude = jnp.sqrt(grad_x * grad_x + grad_y * grad_y + grad_z * grad_z)
    limited = jnp.maximum(magnitude, grad_floor)
    flow_x = -grad_x / limited
    flow_y = -grad_y / limited
    flow_z = -grad_z / limited
    div_x = 0.5 * (flow_x[2:, 1:-1] - flow_x[:-2, 1:-1])
    div_y = 0.5 * (flow_y[1:-1, 2:] - flow_y[1:-1, :-2])
    div_z = central_z(flow_z[1:-1, 1:-1])
    return div_x + div_y + div_z


def per_device(sources, labels):
    count_x, count_y, length = sources.shape
    span = length // lax.axis_size(ALL)
    heat_time = (length / 8.0) ** 2
    grad_floor = 0.04 / heat_time
    scale = 1.0 / float(length) ** 3
    cas = cas_table(length)
    wave = jnp.arange(length, dtype=jnp.int32)
    wave_z = lax.axis_index(ALL) * span + jnp.arange(span, dtype=jnp.int32)
    laplace = (
        eigen(wave, length)[None, :, None] + eigen(wave, length)[None, None, :]
    ) + eigen(wave_z, length)[:, None, None]
    anchor = (wave_z[:, None, None] == 0) & (wave[None, :, None] == 0) & (wave[None, None, :] == 0)

    heat_filter = 1.0 + heat_time * laplace
    laplace_safe = jnp.where(anchor, 1.0, laplace)
    cas_x, cas_y = lax.optimization_barrier(
        (
            cas_columns(length, window_positions(length, count_x, 2)),
            cas_columns(length, window_positions(length, count_y, 4)),
        )
    )
    source = sources.astype(jnp.float32)
    spectrum = planes_forward(to_planes(source, cas), cas)
    padded = to_pencil_with_halo(spectrum / heat_filter * scale, cas, cas_x, cas_y)
    divergence = divergence_of_flow(padded[:, 2:-2], grad_floor)

    div_spectrum = planes_forward(to_planes(divergence, cas), cas)
    potential_spectrum = jnp.where(anchor, 0.0, -div_spectrum / laplace_safe) * scale
    potential = to_pencil(potential_spectrum, cas, count_x, count_y)
    signs = (2 * labels - 1).astype(jnp.float32)
    return signs * potential


def solution(mesh):
    return jax.shard_map(
        per_device,
        mesh=mesh,
        in_specs=(P("wide", "narrow", None), P("wide", "narrow", None)),
        out_specs=P("wide", "narrow", None),
        check_vma=False,
    )
```

```python
import math

import jax
import jax.numpy as jnp
from jax import lax
from jax.sharding import PartitionSpec as P

matmul_precision = lax.Precision.HIGH
ALL = ("narrow", "wide")


def cas_table(length):
    positions = jnp.arange(length, dtype=jnp.int32)
    phase_steps = positions[:, None] * positions[None, :] % length
    angles = phase_steps.astype(jnp.float32) * (2.0 * math.pi / length)
    return jnp.cos(angles) + jnp.sin(angles)


def cas_columns(length, positions):
    wavenumbers = jnp.arange(length, dtype=jnp.int32).reshape((length,) + (1,) * positions.ndim)
    phase_steps = wavenumbers * positions[None] % length
    angles = phase_steps.astype(jnp.float32) * (2.0 * math.pi / length)
    return jnp.cos(angles) + jnp.sin(angles)


def window_positions(length, count, width):
    blocks = length // count
    starts = jnp.arange(blocks, dtype=jnp.int32)[:, None] * count - width
    return (starts + jnp.arange(count + 2 * width, dtype=jnp.int32)[None, :]) % length


def eigen(wavenumber, length):
    angles = wavenumber.astype(jnp.float32) * (2.0 * math.pi / length)
    return 2.0 - 2.0 * jnp.cos(angles)


def to_planes(pencil, cas):
    count_x, count_y, length = pencil.shape
    wide = lax.axis_size("wide")
    narrow = lax.axis_size("narrow")
    span = length // (wide * narrow)
    along_z = jnp.einsum("xyz,zk->kxy", pencil, cas, precision=matmul_precision)
    arrived = lax.all_to_all(along_z.reshape(wide * narrow, span, count_x, count_y), ALL, 0, 0)
    arrived = arrived.reshape(narrow, wide, span, count_x, count_y)
    along_y = jnp.einsum(
        "qwkxy,qyl->kwxl", arrived, cas.reshape(narrow, count_y, length), precision=matmul_precision
    )
    return along_y.reshape(span, wide * count_x, length)


def to_pencil(planes, cas, count_x, count_y):
    span, _, _ = planes.shape
    wide = lax.axis_size("wide")
    narrow = lax.axis_size("narrow")
    send = planes.reshape(span, wide, count_x, narrow, count_y).transpose(3, 1, 0, 2, 4)
    arrived = lax.all_to_all(send.reshape(wide * narrow, span, count_x, count_y), ALL, 0, 0)
    spectrum = arrived.reshape(wide * narrow * span, count_x, count_y)
    return jnp.einsum("kxy,kz->xyz", spectrum, cas, precision=matmul_precision)


def to_pencil_with_halo(spectrum, cas, cas_x, cas_y):
    span, length, _ = spectrum.shape
    _, wide, padded_x = cas_x.shape
    _, narrow, padded_y = cas_y.shape
    along_x = jnp.einsum("kml,mwi->kwil", spectrum, cas_x, precision=matmul_precision)
    windows = jnp.einsum("kwil,lqj->qwkij", along_x, cas_y, precision=matmul_precision)
    send = windows.reshape(wide * narrow, span * padded_x * padded_y)
    arrived = lax.all_to_all(send, ALL, 0, 0)
    spectrum_z = arrived.reshape(wide * narrow * span, padded_x * padded_y)
    values = jnp.einsum("kr,kz->rz", spectrum_z, cas, precision=matmul_precision)
    return values.reshape(padded_x, padded_y, length)


def planes_forward(along_y, cas):
    return jnp.einsum("kxl,xm->kml", along_y, cas, precision=matmul_precision)


def planes_inverse(spectrum, cas):
    along_x = jnp.einsum("kml,mx->kxl", spectrum, cas, precision=matmul_precision)
    return jnp.einsum("kxl,ly->kxy", along_x, cas, precision=matmul_precision)


def central_z(values):
    return 0.5 * (jnp.roll(values, -1, 2) - jnp.roll(values, 1, 2))


def divergence_of_flow(heat, grad_floor):
    inner = heat[1:-1, 1:-1]
    grad_x = 0.5 * (heat[2:, 1:-1] - heat[:-2, 1:-1])
    grad_y = 0.5 * (heat[1:-1, 2:] - heat[1:-1, :-2])
    grad_z = central_z(inner)
    magnitude = jnp.sqrt(grad_x * grad_x + grad_y * grad_y + grad_z * grad_z)
    limited = jnp.maximum(magnitude, grad_floor)
    flow_x = -grad_x / limited
    flow_y = -grad_y / limited
    flow_z = -grad_z / limited
    div_x = 0.5 * (flow_x[2:, 1:-1] - flow_x[:-2, 1:-1])
    div_y = 0.5 * (flow_y[1:-1, 2:] - flow_y[1:-1, :-2])
    div_z = central_z(flow_z[1:-1, 1:-1])
    return div_x + div_y + div_z


def per_device(sources, labels):
    count_x, count_y, length = sources.shape
    span = length // lax.axis_size(ALL)
    heat_time = (length / 8.0) ** 2
    grad_floor = 0.04 / heat_time
    scale = 1.0 / float(length) ** 3
    cas = cas_table(length)
    wave = jnp.arange(length, dtype=jnp.int32)
    wave_z = lax.axis_index(ALL) * span + jnp.arange(span, dtype=jnp.int32)
    laplace = (
        eigen(wave, length)[None, :, None] + eigen(wave, length)[None, None, :]
    ) + eigen(wave_z, length)[:, None, None]
    anchor = (wave_z[:, None, None] == 0) & (wave[None, :, None] == 0) & (wave[None, None, :] == 0)

    heat_filter = 1.0 + heat_time * laplace
    laplace_safe = jnp.where(anchor, 1.0, laplace)
    cas_x, cas_y = lax.optimization_barrier(
        (
            cas_columns(length, window_positions(length, count_x, 2)),
            cas_columns(length, window_positions(length, count_y, 4)),
        )
    )
    source = sources.astype(jnp.float32)
    spectrum = planes_forward(to_planes(source, cas), cas)
    padded = to_pencil_with_halo(spectrum / heat_filter * scale, cas, cas_x, cas_y)
    divergence = divergence_of_flow(padded[:, 2:-2], grad_floor)

    div_spectrum = planes_forward(to_planes(divergence, cas), cas)
    potential_spectrum = jnp.where(anchor, 0.0, -div_spectrum / laplace_safe) * scale
    potential = to_pencil(planes_inverse(potential_spectrum, cas), cas, count_x, count_y)
    signs = (2 * labels - 1).astype(jnp.float32)
    return signs * potential


def solution(mesh):
    return jax.shard_map(
        per_device,
        mesh=mesh,
        in_specs=(P("wide", "narrow", None), P("wide", "narrow", None)),
        out_specs=P("wide", "narrow", None),
        check_vma=False,
    )
```

```python
import math

import jax
import jax.numpy as jnp
from jax import lax
from jax.sharding import PartitionSpec as P

matmul_precision = lax.Precision.HIGH
ALL = ("wide", "narrow")


def cas_table(length):
    positions = jnp.arange(length, dtype=jnp.int32)
    phase_steps = positions[:, None] * positions[None, :] % length
    angles = phase_steps.astype(jnp.float32) * (2.0 * math.pi / length)
    return jnp.cos(angles) + jnp.sin(angles)


def cas_columns(length, positions):
    wavenumbers = jnp.arange(length, dtype=jnp.int32).reshape((length,) + (1,) * positions.ndim)
    phase_steps = wavenumbers * positions[None] % length
    angles = phase_steps.astype(jnp.float32) * (2.0 * math.pi / length)
    return jnp.cos(angles) + jnp.sin(angles)


def window_positions(length, count, width):
    blocks = length // count
    starts = jnp.arange(blocks, dtype=jnp.int32)[:, None] * count - width
    return (starts + jnp.arange(count + 2 * width, dtype=jnp.int32)[None, :]) % length


def eigen(wavenumber, length):
    angles = wavenumber.astype(jnp.float32) * (2.0 * math.pi / length)
    return 2.0 - 2.0 * jnp.cos(angles)


def exchange(blocks):
    shape = blocks.shape
    size = math.prod(shape[1:])
    if size % 1024 == 0:
        blocks = blocks.reshape(shape[0], size // 128, 128)
    return lax.all_to_all(blocks, ALL, 0, 0).reshape(shape)


def to_planes(pencil, cas):
    count_x, count_y, length = pencil.shape
    wide = lax.axis_size("wide")
    narrow = lax.axis_size("narrow")
    span = length // (wide * narrow)
    along_z = jnp.einsum("xyz,zk->kxy", pencil, cas, precision=matmul_precision)
    arrived = exchange(along_z.reshape(wide * narrow, span, count_x, count_y))
    arrived = arrived.reshape(wide, narrow, span, count_x, count_y)
    along_y = jnp.einsum(
        "wqkxy,qyl->kwxl", arrived, cas.reshape(narrow, count_y, length), precision=matmul_precision
    )
    return along_y.reshape(span, wide * count_x, length)


def to_pencil(planes, cas, count_x, count_y):
    span, _, _ = planes.shape
    wide = lax.axis_size("wide")
    narrow = lax.axis_size("narrow")
    send = planes.reshape(span, wide, count_x, narrow, count_y).transpose(1, 3, 0, 2, 4)
    arrived = exchange(send.reshape(wide * narrow, span, count_x, count_y))
    spectrum = arrived.reshape(wide * narrow * span, count_x, count_y)
    return jnp.einsum("kxy,kz->xyz", spectrum, cas, precision=matmul_precision)


def to_pencil_with_halo(spectrum, cas, cas_x, cas_y):
    span, length, _ = spectrum.shape
    _, wide, padded_x = cas_x.shape
    _, narrow, padded_y = cas_y.shape
    along_x = jnp.einsum("kml,mwi->kwil", spectrum, cas_x, precision=matmul_precision)
    windows = jnp.einsum("kwil,lqj->wqkij", along_x, cas_y, precision=matmul_precision)
    send = windows.reshape(wide * narrow, span * padded_x * padded_y)
    arrived = lax.all_to_all(send, ALL, 0, 0)
    spectrum_z = arrived.reshape(wide * narrow * span, padded_x * padded_y)
    values = jnp.einsum("kr,kz->rz", spectrum_z, cas, precision=matmul_precision)
    return values.reshape(padded_x, padded_y, length)


def planes_forward(along_y, cas):
    return jnp.einsum("kxl,xm->kml", along_y, cas, precision=matmul_precision)


def planes_inverse(spectrum, cas):
    along_x = jnp.einsum("kml,mx->kxl", spectrum, cas, precision=matmul_precision)
    return jnp.einsum("kxl,ly->kxy", along_x, cas, precision=matmul_precision)


def central_z(values):
    return 0.5 * (jnp.roll(values, -1, 2) - jnp.roll(values, 1, 2))


def divergence_of_flow(heat, grad_floor):
    inner = heat[1:-1, 1:-1]
    grad_x = 0.5 * (heat[2:, 1:-1] - heat[:-2, 1:-1])
    grad_y = 0.5 * (heat[1:-1, 2:] - heat[1:-1, :-2])
    grad_z = central_z(inner)
    magnitude = jnp.sqrt(grad_x * grad_x + grad_y * grad_y + grad_z * grad_z)
    limited = jnp.maximum(magnitude, grad_floor)
    flow_x = -grad_x / limited
    flow_y = -grad_y / limited
    flow_z = -grad_z / limited
    div_x = 0.5 * (flow_x[2:, 1:-1] - flow_x[:-2, 1:-1])
    div_y = 0.5 * (flow_y[1:-1, 2:] - flow_y[1:-1, :-2])
    div_z = central_z(flow_z[1:-1, 1:-1])
    return div_x + div_y + div_z


def per_device(sources, labels):
    count_x, count_y, length = sources.shape
    span = length // lax.axis_size(ALL)
    heat_time = (length / 8.0) ** 2
    grad_floor = 0.04 / heat_time
    scale = 1.0 / float(length) ** 3
    cas = cas_table(length)
    wave = jnp.arange(length, dtype=jnp.int32)
    wave_z = lax.axis_index(ALL) * span + jnp.arange(span, dtype=jnp.int32)
    laplace = (
        eigen(wave, length)[None, :, None] + eigen(wave, length)[None, None, :]
    ) + eigen(wave_z, length)[:, None, None]
    anchor = (wave_z[:, None, None] == 0) & (wave[None, :, None] == 0) & (wave[None, None, :] == 0)

    heat_filter = 1.0 + heat_time * laplace
    laplace_safe = jnp.where(anchor, 1.0, laplace)
    cas_x, cas_y = lax.optimization_barrier(
        (
            cas_columns(length, window_positions(length, count_x, 2)),
            cas_columns(length, window_positions(length, count_y, 4)),
        )
    )
    source = sources.astype(jnp.float32)
    spectrum = planes_forward(to_planes(source, cas), cas)
    padded = to_pencil_with_halo(spectrum / heat_filter * scale, cas, cas_x, cas_y)
    divergence = divergence_of_flow(padded[:, 2:-2], grad_floor)

    div_spectrum = planes_forward(to_planes(divergence, cas), cas)
    potential_spectrum = jnp.where(anchor, 0.0, -div_spectrum / laplace_safe) * scale
    potential = to_pencil(planes_inverse(potential_spectrum, cas), cas, count_x, count_y)
    signs = (2 * labels - 1).astype(jnp.float32)
    return signs * potential


def solution(mesh):
    return jax.shard_map(
        per_device,
        mesh=mesh,
        in_specs=(P("wide", "narrow", None), P("wide", "narrow", None)),
        out_specs=P("wide", "narrow", None),
        check_vma=False,
    )
```

```python
import math

import jax
import jax.numpy as jnp
from jax import lax
from jax.sharding import PartitionSpec as P

matmul_precision = lax.Precision.HIGH
ALL = ("wide", "narrow")


def cas_table(length):
    positions = jnp.arange(length, dtype=jnp.int32)
    phase_steps = positions[:, None] * positions[None, :] % length
    angles = phase_steps.astype(jnp.float32) * (2.0 * math.pi / length)
    return jnp.cos(angles) + jnp.sin(angles)


def cas_columns(length, positions):
    wavenumbers = jnp.arange(length, dtype=jnp.int32).reshape((length,) + (1,) * positions.ndim)
    phase_steps = wavenumbers * positions[None] % length
    angles = phase_steps.astype(jnp.float32) * (2.0 * math.pi / length)
    return jnp.cos(angles) + jnp.sin(angles)


def window_positions(length, count, width):
    blocks = length // count
    starts = jnp.arange(blocks, dtype=jnp.int32)[:, None] * count - width
    return (starts + jnp.arange(count + 2 * width, dtype=jnp.int32)[None, :]) % length


def eigen(wavenumber, length):
    angles = wavenumber.astype(jnp.float32) * (2.0 * math.pi / length)
    return 2.0 - 2.0 * jnp.cos(angles)


def exchange(blocks):
    shape = blocks.shape
    size = math.prod(shape[1:])
    tiles = -(-size // 1024)
    flat = blocks.reshape(shape[0], size)
    if tiles * 1024 != size:
        flat = jnp.pad(flat, ((0, 0), (0, tiles * 1024 - size)))
    arrived = lax.all_to_all(flat.reshape(shape[0], tiles * 8, 128), ALL, 0, 0)
    return arrived.reshape(shape[0], tiles * 1024)[:, :size].reshape(shape)


def to_planes(pencil, cas):
    count_x, count_y, length = pencil.shape
    wide = lax.axis_size("wide")
    narrow = lax.axis_size("narrow")
    span = length // (wide * narrow)
    along_z = jnp.einsum("xyz,zk->kxy", pencil, cas, precision=matmul_precision)
    arrived = exchange(along_z.reshape(wide * narrow, span, count_x, count_y))
    arrived = arrived.reshape(wide, narrow, span, count_x, count_y)
    along_y = jnp.einsum(
        "wqkxy,qyl->kwxl", arrived, cas.reshape(narrow, count_y, length), precision=matmul_precision
    )
    return along_y.reshape(span, wide * count_x, length)


def to_pencil(planes, cas, count_x, count_y):
    span, _, _ = planes.shape
    wide = lax.axis_size("wide")
    narrow = lax.axis_size("narrow")
    send = planes.reshape(span, wide, count_x, narrow, count_y).transpose(1, 3, 0, 2, 4)
    arrived = exchange(send.reshape(wide * narrow, span, count_x, count_y))
    spectrum = arrived.reshape(wide * narrow * span, count_x, count_y)
    return jnp.einsum("kxy,kz->xyz", spectrum, cas, precision=matmul_precision)


def to_pencil_with_halo(spectrum, cas, cas_x, cas_y):
    span, length, _ = spectrum.shape
    _, wide, padded_x = cas_x.shape
    _, narrow, padded_y = cas_y.shape
    along_x = jnp.einsum("kml,mwi->kwil", spectrum, cas_x, precision=matmul_precision)
    windows = jnp.einsum("kwil,lqj->wqkij", along_x, cas_y, precision=matmul_precision)
    arrived = exchange(windows.reshape(wide * narrow, span * padded_x * padded_y))
    spectrum_z = arrived.reshape(wide * narrow * span, padded_x * padded_y)
    values = jnp.einsum("kr,kz->rz", spectrum_z, cas, precision=matmul_precision)
    return values.reshape(padded_x, padded_y, length)


def planes_forward(along_y, cas):
    return jnp.einsum("kxl,xm->kml", along_y, cas, precision=matmul_precision)


def planes_inverse(spectrum, cas):
    along_x = jnp.einsum("kml,mx->kxl", spectrum, cas, precision=matmul_precision)
    return jnp.einsum("kxl,ly->kxy", along_x, cas, precision=matmul_precision)


def central_z(values):
    return 0.5 * (jnp.roll(values, -1, 2) - jnp.roll(values, 1, 2))


def divergence_of_flow(heat, grad_floor):
    inner = heat[1:-1, 1:-1]
    grad_x = 0.5 * (heat[2:, 1:-1] - heat[:-2, 1:-1])
    grad_y = 0.5 * (heat[1:-1, 2:] - heat[1:-1, :-2])
    grad_z = central_z(inner)
    magnitude = jnp.sqrt(grad_x * grad_x + grad_y * grad_y + grad_z * grad_z)
    limited = jnp.maximum(magnitude, grad_floor)
    flow_x = -grad_x / limited
    flow_y = -grad_y / limited
    flow_z = -grad_z / limited
    div_x = 0.5 * (flow_x[2:, 1:-1] - flow_x[:-2, 1:-1])
    div_y = 0.5 * (flow_y[1:-1, 2:] - flow_y[1:-1, :-2])
    div_z = central_z(flow_z[1:-1, 1:-1])
    return div_x + div_y + div_z


def per_device(sources, labels):
    count_x, count_y, length = sources.shape
    span = length // lax.axis_size(ALL)
    heat_time = (length / 8.0) ** 2
    grad_floor = 0.04 / heat_time
    scale = 1.0 / float(length) ** 3
    cas = cas_table(length)
    wave = jnp.arange(length, dtype=jnp.int32)
    wave_z = lax.axis_index(ALL) * span + jnp.arange(span, dtype=jnp.int32)
    laplace = (
        eigen(wave, length)[None, :, None] + eigen(wave, length)[None, None, :]
    ) + eigen(wave_z, length)[:, None, None]
    anchor = (wave_z[:, None, None] == 0) & (wave[None, :, None] == 0) & (wave[None, None, :] == 0)

    heat_filter = 1.0 + heat_time * laplace
    laplace_safe = jnp.where(anchor, 1.0, laplace)
    cas_x, cas_y = lax.optimization_barrier(
        (
            cas_columns(length, window_positions(length, count_x, 2)),
            cas_columns(length, window_positions(length, count_y, 4)),
        )
    )
    source = sources.astype(jnp.float32)
    spectrum = planes_forward(to_planes(source, cas), cas)
    padded = to_pencil_with_halo(spectrum / heat_filter * scale, cas, cas_x, cas_y)
    divergence = divergence_of_flow(padded[:, 2:-2], grad_floor)

    div_spectrum = planes_forward(to_planes(divergence, cas), cas)
    potential_spectrum = jnp.where(anchor, 0.0, -div_spectrum / laplace_safe) * scale
    potential = to_pencil(planes_inverse(potential_spectrum, cas), cas, count_x, count_y)
    signs = (2 * labels - 1).astype(jnp.float32)
    return signs * potential


def solution(mesh):
    return jax.shard_map(
        per_device,
        mesh=mesh,
        in_specs=(P("wide", "narrow", None), P("wide", "narrow", None)),
        out_specs=P("wide", "narrow", None),
        check_vma=False,
    )
```

```python
import math

import jax
import jax.numpy as jnp
from jax import lax
from jax.sharding import PartitionSpec as P

matmul_precision = lax.Precision.HIGH
ALL = ("wide", "narrow")


def cas_table(length):
    positions = jnp.arange(length, dtype=jnp.int32)
    phase_steps = positions[:, None] * positions[None, :] % length
    angles = phase_steps.astype(jnp.float32) * (2.0 * math.pi / length)
    return jnp.cos(angles) + jnp.sin(angles)


def cas_columns(length, positions):
    wavenumbers = jnp.arange(length, dtype=jnp.int32).reshape((length,) + (1,) * positions.ndim)
    phase_steps = wavenumbers * positions[None] % length
    angles = phase_steps.astype(jnp.float32) * (2.0 * math.pi / length)
    return jnp.cos(angles) + jnp.sin(angles)


def window_positions(length, count, width):
    blocks = length // count
    starts = jnp.arange(blocks, dtype=jnp.int32)[:, None] * count - width
    return (starts + jnp.arange(count + 2 * width, dtype=jnp.int32)[None, :]) % length


def eigen(wavenumber, length):
    angles = wavenumber.astype(jnp.float32) * (2.0 * math.pi / length)
    return 2.0 - 2.0 * jnp.cos(angles)


def exchange(blocks):
    shape = blocks.shape
    size = math.prod(shape[1:])
    tiles = -(-size // 1024)
    flat = blocks.reshape(shape[0], size)
    if tiles * 1024 != size:
        flat = jnp.pad(flat, ((0, 0), (0, tiles * 1024 - size)))
    arrived = lax.all_to_all(flat.reshape(shape[0], tiles * 8, 128), ALL, 0, 0)
    return arrived.reshape(shape[0], tiles * 1024)[:, :size].reshape(shape)


def to_planes(pencil, cas):
    count_x, count_y, length = pencil.shape
    wide = lax.axis_size("wide")
    narrow = lax.axis_size("narrow")
    span = length // (wide * narrow)
    along_z = jnp.einsum("xyz,zk->kxy", pencil, cas, precision=matmul_precision)
    arrived = exchange(along_z.reshape(wide * narrow, span, count_x, count_y))
    arrived = arrived.reshape(wide, narrow, span, count_x, count_y)
    along_y = jnp.einsum(
        "wqkxy,qyl->kwxl", arrived, cas.reshape(narrow, count_y, length), precision=matmul_precision
    )
    return along_y.reshape(span, wide * count_x, length)


def to_pencil(planes, cas, count_x, count_y):
    span, _, _ = planes.shape
    wide = lax.axis_size("wide")
    narrow = lax.axis_size("narrow")
    send = planes.reshape(span, wide, count_x, narrow, count_y).transpose(1, 3, 0, 2, 4)
    arrived = exchange(send.reshape(wide * narrow, span, count_x, count_y))
    spectrum = arrived.reshape(wide * narrow * span, count_x, count_y)
    return jnp.einsum("kxy,kz->xyz", spectrum, cas, precision=matmul_precision)


def to_pencil_with_halo(spectrum, cas, cas_x, cas_y):
    span, length, _ = spectrum.shape
    _, wide, padded_x = cas_x.shape
    _, narrow, padded_y = cas_y.shape
    along_x = jnp.einsum("kml,mwi->kwil", spectrum, cas_x, precision=matmul_precision)
    windows = jnp.einsum("kwil,lqj->wqkij", along_x, cas_y, precision=matmul_precision)
    arrived = exchange(windows.reshape(wide * narrow, span * padded_x * padded_y))
    spectrum_z = arrived.reshape(wide * narrow * span, padded_x * padded_y)
    values = jnp.einsum("kr,kz->rz", spectrum_z, cas, precision=matmul_precision)
    return values.reshape(padded_x, padded_y, length)


def planes_forward(along_y, cas):
    return jnp.einsum("kxl,xm->kml", along_y, cas, precision=matmul_precision)


def planes_inverse(spectrum, cas):
    along_x = jnp.einsum("kml,mx->kxl", spectrum, cas, precision=matmul_precision)
    return jnp.einsum("kxl,ly->kxy", along_x, cas, precision=matmul_precision)


def central_z(values):
    return 0.5 * (jnp.roll(values, -1, 2) - jnp.roll(values, 1, 2))


def divergence_of_flow(heat, grad_floor):
    inner = heat[1:-1, 1:-1]
    grad_x = 0.5 * (heat[2:, 1:-1] - heat[:-2, 1:-1])
    grad_y = 0.5 * (heat[1:-1, 2:] - heat[1:-1, :-2])
    grad_z = central_z(inner)
    magnitude = jnp.sqrt(grad_x * grad_x + grad_y * grad_y + grad_z * grad_z)
    limited = jnp.maximum(magnitude, grad_floor)
    flow_x = -grad_x / limited
    flow_y = -grad_y / limited
    flow_z = -grad_z / limited
    div_x = 0.5 * (flow_x[2:, 1:-1] - flow_x[:-2, 1:-1])
    div_y = 0.5 * (flow_y[1:-1, 2:] - flow_y[1:-1, :-2])
    div_z = central_z(flow_z[1:-1, 1:-1])
    return div_x + div_y + div_z


def per_device(sources, labels):
    count_x, count_y, length = sources.shape
    span = length // lax.axis_size(ALL)
    heat_time = (length / 8.0) ** 2
    grad_floor = 0.04 / heat_time
    scale = 1.0 / float(length) ** 3
    cas = cas_table(length)
    wave = jnp.arange(length, dtype=jnp.int32)
    wave_z = lax.axis_index(ALL) * span + jnp.arange(span, dtype=jnp.int32)
    laplace = (
        eigen(wave, length)[None, :, None] + eigen(wave, length)[None, None, :]
    ) + eigen(wave_z, length)[:, None, None]
    anchor = (wave_z[:, None, None] == 0) & (wave[None, :, None] == 0) & (wave[None, None, :] == 0)

    heat_filter = 1.0 + heat_time * laplace
    laplace_safe = jnp.where(anchor, 1.0, laplace)
    cas, cas_x, cas_y = lax.optimization_barrier(
        (
            cas,
            cas_columns(length, window_positions(length, count_x, 2)),
            cas_columns(length, window_positions(length, count_y, 4)),
        )
    )
    source = sources.astype(jnp.float32)
    spectrum = planes_forward(to_planes(source, cas), cas)
    padded = to_pencil_with_halo(spectrum / heat_filter * scale, cas, cas_x, cas_y)
    divergence = divergence_of_flow(padded[:, 2:-2], grad_floor)

    div_spectrum = planes_forward(to_planes(divergence, cas), cas)
    potential_spectrum = jnp.where(anchor, 0.0, -div_spectrum / laplace_safe) * scale
    potential = to_pencil(planes_inverse(potential_spectrum, cas), cas, count_x, count_y)
    signs = (2 * labels - 1).astype(jnp.float32)
    return signs * potential


def solution(mesh):
    return jax.shard_map(
        per_device,
        mesh=mesh,
        in_specs=(P("wide", "narrow", None), P("wide", "narrow", None)),
        out_specs=P("wide", "narrow", None),
        check_vma=False,
    )
```

```python
import math

import jax
import jax.numpy as jnp
from jax import lax
from jax.sharding import PartitionSpec as P

matmul_precision = lax.Precision.HIGH
ALL = ("wide", "narrow")


def cas_table(length):
    positions = jnp.arange(length, dtype=jnp.int32)
    phase_steps = positions[:, None] * positions[None, :] % length
    angles = phase_steps.astype(jnp.float32) * (2.0 * math.pi / length)
    return jnp.cos(angles) + jnp.sin(angles)


def cas_columns(length, positions):
    wavenumbers = jnp.arange(length, dtype=jnp.int32).reshape((length,) + (1,) * positions.ndim)
    phase_steps = wavenumbers * positions[None] % length
    angles = phase_steps.astype(jnp.float32) * (2.0 * math.pi / length)
    return jnp.cos(angles) + jnp.sin(angles)


def window_positions(length, count, width):
    blocks = length // count
    starts = jnp.arange(blocks, dtype=jnp.int32)[:, None] * count - width
    return (starts + jnp.arange(count + 2 * width, dtype=jnp.int32)[None, :]) % length


def eigen(wavenumber, length):
    angles = wavenumber.astype(jnp.float32) * (2.0 * math.pi / length)
    return 2.0 - 2.0 * jnp.cos(angles)


def exchange(blocks):
    shape = blocks.shape
    size = math.prod(shape[1:])
    tiles = -(-size // 1024)
    flat = blocks.reshape(shape[0], size)
    if tiles * 1024 != size:
        flat = jnp.pad(flat, ((0, 0), (0, tiles * 1024 - size)))
    arrived = lax.all_to_all(flat.reshape(shape[0], tiles * 8, 128), ALL, 0, 0)
    return arrived.reshape(shape[0], tiles * 1024)[:, :size].reshape(shape)


def to_planes(pencil, cas):
    count_x, count_y, length = pencil.shape
    wide = lax.axis_size("wide")
    narrow = lax.axis_size("narrow")
    span = length // (wide * narrow)
    along_z = jnp.einsum("xyz,zk->kxy", pencil, cas, precision=matmul_precision)
    arrived = exchange(along_z.reshape(wide * narrow, span, count_x, count_y))
    arrived = arrived.reshape(wide, narrow, span, count_x, count_y)
    along_y = jnp.einsum(
        "wqkxy,qyl->kwxl", arrived, cas.reshape(narrow, count_y, length), precision=matmul_precision
    )
    return along_y.reshape(span, wide * count_x, length)


def to_pencil(planes, cas, count_x, count_y):
    span, _, _ = planes.shape
    wide = lax.axis_size("wide")
    narrow = lax.axis_size("narrow")
    send = planes.reshape(span, wide, count_x, narrow, count_y).transpose(1, 3, 0, 2, 4)
    arrived = exchange(send.reshape(wide * narrow, span, count_x, count_y))
    spectrum = arrived.reshape(wide * narrow * span, count_x, count_y)
    return jnp.einsum("kxy,kz->xyz", spectrum, cas, precision=matmul_precision)


def to_pencil_with_halo(spectrum, cas, cas_x, cas_y):
    span, length, _ = spectrum.shape
    _, wide, padded_x = cas_x.shape
    _, narrow, padded_y = cas_y.shape
    along_x = jnp.einsum("kml,mwi->kwil", spectrum, cas_x, precision=matmul_precision)
    windows = jnp.einsum("kwil,lqj->wqkij", along_x, cas_y, precision=matmul_precision)
    arrived = exchange(windows.reshape(wide * narrow, span * padded_x * padded_y))
    spectrum_z = arrived.reshape(wide * narrow * span, padded_x * padded_y)
    values = jnp.einsum("kr,kz->rz", spectrum_z, cas, precision=matmul_precision)
    return values.reshape(padded_x, padded_y, length)


def planes_forward(along_y, cas):
    return jnp.einsum("kxl,xm->kml", along_y, cas, precision=matmul_precision)


def planes_inverse(spectrum, cas):
    along_x = jnp.einsum("kml,mx->kxl", spectrum, cas, precision=matmul_precision)
    return jnp.einsum("kxl,ly->kxy", along_x, cas, precision=matmul_precision)


def central_z(values):
    return 0.5 * (jnp.roll(values, -1, 2) - jnp.roll(values, 1, 2))


def divergence_of_flow(heat, grad_floor):
    inner = heat[1:-1, 1:-1]
    grad_x = 0.5 * (heat[2:, 1:-1] - heat[:-2, 1:-1])
    grad_y = 0.5 * (heat[1:-1, 2:] - heat[1:-1, :-2])
    grad_z = central_z(inner)
    magnitude = jnp.sqrt(grad_x * grad_x + grad_y * grad_y + grad_z * grad_z)
    limited = jnp.maximum(magnitude, grad_floor)
    flow_x = -grad_x / limited
    flow_y = -grad_y / limited
    flow_z = -grad_z / limited
    div_x = 0.5 * (flow_x[2:, 1:-1] - flow_x[:-2, 1:-1])
    div_y = 0.5 * (flow_y[1:-1, 2:] - flow_y[1:-1, :-2])
    div_z = central_z(flow_z[1:-1, 1:-1])
    return div_x + div_y + div_z


def per_device(sources, labels):
    count_x, count_y, length = sources.shape
    span = length // lax.axis_size(ALL)
    heat_time = (length / 8.0) ** 2
    grad_floor = 0.04 / heat_time
    scale = 1.0 / float(length) ** 3
    cas = cas_table(length)
    wave = jnp.arange(length, dtype=jnp.int32)
    wave_z = lax.axis_index(ALL) * span + jnp.arange(span, dtype=jnp.int32)
    laplace = (
        eigen(wave, length)[None, :, None] + eigen(wave, length)[None, None, :]
    ) + eigen(wave_z, length)[:, None, None]
    anchor = (wave_z[:, None, None] == 0) & (wave[None, :, None] == 0) & (wave[None, None, :] == 0)

    heat_filter = 1.0 + heat_time * laplace
    laplace_safe = jnp.where(anchor, 1.0, laplace)
    cas = lax.optimization_barrier(cas)
    cas_x, cas_y = lax.optimization_barrier(
        (
            cas_columns(length, window_positions(length, count_x, 2)),
            cas_columns(length, window_positions(length, count_y, 4)),
        )
    )
    source = sources.astype(jnp.float32)
    spectrum = planes_forward(to_planes(source, cas), cas)
    padded = to_pencil_with_halo(spectrum / heat_filter * scale, cas, cas_x, cas_y)
    divergence = divergence_of_flow(padded[:, 2:-2], grad_floor)

    div_spectrum = planes_forward(to_planes(divergence, cas), cas)
    potential_spectrum = jnp.where(anchor, 0.0, -div_spectrum / laplace_safe) * scale
    potential = to_pencil(planes_inverse(potential_spectrum, cas), cas, count_x, count_y)
    signs = (2 * labels - 1).astype(jnp.float32)
    return signs * potential


def solution(mesh):
    return jax.shard_map(
        per_device,
        mesh=mesh,
        in_specs=(P("wide", "narrow", None), P("wide", "narrow", None)),
        out_specs=P("wide", "narrow", None),
        check_vma=False,
    )
```

```python
import math

import jax
import numpy as np
import jax.numpy as jnp
from jax import lax
from jax.sharding import PartitionSpec as P

matmul_precision = lax.Precision.HIGH
ALL = ("wide", "narrow")


def cas_table(length):
    positions = np.arange(length, dtype=np.int64)
    angles = (positions[:, None] * positions[None, :] % length) * (2.0 * math.pi / length)
    return jnp.asarray((np.cos(angles) + np.sin(angles)).astype(np.float32))


def cas_columns(length, positions):
    wavenumbers = jnp.arange(length, dtype=jnp.int32).reshape((length,) + (1,) * positions.ndim)
    phase_steps = wavenumbers * positions[None] % length
    angles = phase_steps.astype(jnp.float32) * (2.0 * math.pi / length)
    return jnp.cos(angles) + jnp.sin(angles)


def window_positions(length, count, width):
    blocks = length // count
    starts = jnp.arange(blocks, dtype=jnp.int32)[:, None] * count - width
    return (starts + jnp.arange(count + 2 * width, dtype=jnp.int32)[None, :]) % length


def eigen(wavenumber, length):
    angles = wavenumber.astype(jnp.float32) * (2.0 * math.pi / length)
    return 2.0 - 2.0 * jnp.cos(angles)


def exchange(blocks):
    shape = blocks.shape
    size = math.prod(shape[1:])
    tiles = -(-size // 1024)
    flat = blocks.reshape(shape[0], size)
    if tiles * 1024 != size:
        flat = jnp.pad(flat, ((0, 0), (0, tiles * 1024 - size)))
    arrived = lax.all_to_all(flat.reshape(shape[0], tiles * 8, 128), ALL, 0, 0)
    return arrived.reshape(shape[0], tiles * 1024)[:, :size].reshape(shape)


def to_planes(pencil, cas):
    count_x, count_y, length = pencil.shape
    wide = lax.axis_size("wide")
    narrow = lax.axis_size("narrow")
    span = length // (wide * narrow)
    along_z = jnp.einsum("xyz,zk->kxy", pencil, cas, precision=matmul_precision)
    arrived = exchange(along_z.reshape(wide * narrow, span, count_x, count_y))
    arrived = arrived.reshape(wide, narrow, span, count_x, count_y)
    along_y = jnp.einsum(
        "wqkxy,qyl->kwxl", arrived, cas.reshape(narrow, count_y, length), precision=matmul_precision
    )
    return along_y.reshape(span, wide * count_x, length)


def to_pencil(planes, cas, count_x, count_y):
    span, _, _ = planes.shape
    wide = lax.axis_size("wide")
    narrow = lax.axis_size("narrow")
    send = planes.reshape(span, wide, count_x, narrow, count_y).transpose(1, 3, 0, 2, 4)
    arrived = exchange(send.reshape(wide * narrow, span, count_x, count_y))
    spectrum = arrived.reshape(wide * narrow * span, count_x, count_y)
    return jnp.einsum("kxy,kz->xyz", spectrum, cas, precision=matmul_precision)


def to_pencil_with_halo(spectrum, cas, cas_x, cas_y):
    span, length, _ = spectrum.shape
    _, wide, padded_x = cas_x.shape
    _, narrow, padded_y = cas_y.shape
    along_x = jnp.einsum("kml,mwi->kwil", spectrum, cas_x, precision=matmul_precision)
    windows = jnp.einsum("kwil,lqj->wqkij", along_x, cas_y, precision=matmul_precision)
    arrived = exchange(windows.reshape(wide * narrow, span * padded_x * padded_y))
    spectrum_z = arrived.reshape(wide * narrow * span, padded_x * padded_y)
    values = jnp.einsum("kr,kz->rz", spectrum_z, cas, precision=matmul_precision)
    return values.reshape(padded_x, padded_y, length)


def planes_forward(along_y, cas):
    return jnp.einsum("kxl,xm->kml", along_y, cas, precision=matmul_precision)


def planes_inverse(spectrum, cas):
    along_x = jnp.einsum("kml,mx->kxl", spectrum, cas, precision=matmul_precision)
    return jnp.einsum("kxl,ly->kxy", along_x, cas, precision=matmul_precision)


def central_z(values):
    return 0.5 * (jnp.roll(values, -1, 2) - jnp.roll(values, 1, 2))


def divergence_of_flow(heat, grad_floor):
    inner = heat[1:-1, 1:-1]
    grad_x = 0.5 * (heat[2:, 1:-1] - heat[:-2, 1:-1])
    grad_y = 0.5 * (heat[1:-1, 2:] - heat[1:-1, :-2])
    grad_z = central_z(inner)
    magnitude = jnp.sqrt(grad_x * grad_x + grad_y * grad_y + grad_z * grad_z)
    limited = jnp.maximum(magnitude, grad_floor)
    flow_x = -grad_x / limited
    flow_y = -grad_y / limited
    flow_z = -grad_z / limited
    div_x = 0.5 * (flow_x[2:, 1:-1] - flow_x[:-2, 1:-1])
    div_y = 0.5 * (flow_y[1:-1, 2:] - flow_y[1:-1, :-2])
    div_z = central_z(flow_z[1:-1, 1:-1])
    return div_x + div_y + div_z


def per_device(sources, labels):
    count_x, count_y, length = sources.shape
    span = length // lax.axis_size(ALL)
    heat_time = (length / 8.0) ** 2
    grad_floor = 0.04 / heat_time
    scale = 1.0 / float(length) ** 3
    cas = cas_table(length)
    wave = jnp.arange(length, dtype=jnp.int32)
    wave_z = lax.axis_index(ALL) * span + jnp.arange(span, dtype=jnp.int32)
    laplace = (
        eigen(wave, length)[None, :, None] + eigen(wave, length)[None, None, :]
    ) + eigen(wave_z, length)[:, None, None]
    anchor = (wave_z[:, None, None] == 0) & (wave[None, :, None] == 0) & (wave[None, None, :] == 0)

    heat_filter = 1.0 + heat_time * laplace
    laplace_safe = jnp.where(anchor, 1.0, laplace)
    cas_x, cas_y = lax.optimization_barrier(
        (
            cas_columns(length, window_positions(length, count_x, 2)),
            cas_columns(length, window_positions(length, count_y, 4)),
        )
    )
    source = sources.astype(jnp.float32)
    spectrum = planes_forward(to_planes(source, cas), cas)
    padded = to_pencil_with_halo(spectrum / heat_filter * scale, cas, cas_x, cas_y)
    divergence = divergence_of_flow(padded[:, 2:-2], grad_floor)

    div_spectrum = planes_forward(to_planes(divergence, cas), cas)
    potential_spectrum = jnp.where(anchor, 0.0, -div_spectrum / laplace_safe) * scale
    potential = to_pencil(planes_inverse(potential_spectrum, cas), cas, count_x, count_y)
    signs = (2 * labels - 1).astype(jnp.float32)
    return signs * potential


def solution(mesh):
    return jax.shard_map(
        per_device,
        mesh=mesh,
        in_specs=(P("wide", "narrow", None), P("wide", "narrow", None)),
        out_specs=P("wide", "narrow", None),
        check_vma=False,
    )
```

```python
import math

import jax
import numpy as np
import jax.numpy as jnp
from jax import lax
from jax.sharding import PartitionSpec as P

matmul_precision = lax.Precision.HIGH
ALL = ("wide", "narrow")


def cas_table(length):
    positions = np.arange(length, dtype=np.int64)
    angles = (positions[:, None] * positions[None, :] % length) * (2.0 * math.pi / length)
    return jnp.asarray((np.cos(angles) + np.sin(angles)).astype(np.float32))


def cas_columns(length, positions):
    wavenumbers = np.arange(length, dtype=np.int64).reshape((length,) + (1,) * positions.ndim)
    angles = (wavenumbers * positions[None] % length) * (2.0 * math.pi / length)
    return jnp.asarray((np.cos(angles) + np.sin(angles)).astype(np.float32))


def window_positions(length, count, width):
    blocks = length // count
    starts = np.arange(blocks, dtype=np.int64)[:, None] * count - width
    return (starts + np.arange(count + 2 * width, dtype=np.int64)[None, :]) % length


def eigen(wavenumber, length):
    angles = wavenumber.astype(jnp.float32) * (2.0 * math.pi / length)
    return 2.0 - 2.0 * jnp.cos(angles)


def exchange(blocks):
    shape = blocks.shape
    size = math.prod(shape[1:])
    tiles = -(-size // 1024)
    flat = blocks.reshape(shape[0], size)
    if tiles * 1024 != size:
        flat = jnp.pad(flat, ((0, 0), (0, tiles * 1024 - size)))
    arrived = lax.all_to_all(flat.reshape(shape[0], tiles * 8, 128), ALL, 0, 0)
    return arrived.reshape(shape[0], tiles * 1024)[:, :size].reshape(shape)


def to_planes(pencil, cas):
    count_x, count_y, length = pencil.shape
    wide = lax.axis_size("wide")
    narrow = lax.axis_size("narrow")
    span = length // (wide * narrow)
    along_z = jnp.einsum("xyz,zk->kxy", pencil, cas, precision=matmul_precision)
    arrived = exchange(along_z.reshape(wide * narrow, span, count_x, count_y))
    arrived = arrived.reshape(wide, narrow, span, count_x, count_y)
    along_y = jnp.einsum(
        "wqkxy,qyl->kwxl", arrived, cas.reshape(narrow, count_y, length), precision=matmul_precision
    )
    return along_y.reshape(span, wide * count_x, length)


def to_pencil(planes, cas, count_x, count_y):
    span, _, _ = planes.shape
    wide = lax.axis_size("wide")
    narrow = lax.axis_size("narrow")
    send = planes.reshape(span, wide, count_x, narrow, count_y).transpose(1, 3, 0, 2, 4)
    arrived = exchange(send.reshape(wide * narrow, span, count_x, count_y))
    spectrum = arrived.reshape(wide * narrow * span, count_x, count_y)
    return jnp.einsum("kxy,kz->xyz", spectrum, cas, precision=matmul_precision)


def to_pencil_with_halo(spectrum, cas, cas_x, cas_y):
    span, length, _ = spectrum.shape
    _, wide, padded_x = cas_x.shape
    _, narrow, padded_y = cas_y.shape
    along_x = jnp.einsum("kml,mwi->kwil", spectrum, cas_x, precision=matmul_precision)
    windows = jnp.einsum("kwil,lqj->wqkij", along_x, cas_y, precision=matmul_precision)
    arrived = exchange(windows.reshape(wide * narrow, span * padded_x * padded_y))
    spectrum_z = arrived.reshape(wide * narrow * span, padded_x * padded_y)
    values = jnp.einsum("kr,kz->rz", spectrum_z, cas, precision=matmul_precision)
    return values.reshape(padded_x, padded_y, length)


def planes_forward(along_y, cas):
    return jnp.einsum("kxl,xm->kml", along_y, cas, precision=matmul_precision)


def planes_inverse(spectrum, cas):
    along_x = jnp.einsum("kml,mx->kxl", spectrum, cas, precision=matmul_precision)
    return jnp.einsum("kxl,ly->kxy", along_x, cas, precision=matmul_precision)


def central_z(values):
    return 0.5 * (jnp.roll(values, -1, 2) - jnp.roll(values, 1, 2))


def divergence_of_flow(heat, grad_floor):
    inner = heat[1:-1, 1:-1]
    grad_x = 0.5 * (heat[2:, 1:-1] - heat[:-2, 1:-1])
    grad_y = 0.5 * (heat[1:-1, 2:] - heat[1:-1, :-2])
    grad_z = central_z(inner)
    magnitude = jnp.sqrt(grad_x * grad_x + grad_y * grad_y + grad_z * grad_z)
    limited = jnp.maximum(magnitude, grad_floor)
    flow_x = -grad_x / limited
    flow_y = -grad_y / limited
    flow_z = -grad_z / limited
    div_x = 0.5 * (flow_x[2:, 1:-1] - flow_x[:-2, 1:-1])
    div_y = 0.5 * (flow_y[1:-1, 2:] - flow_y[1:-1, :-2])
    div_z = central_z(flow_z[1:-1, 1:-1])
    return div_x + div_y + div_z


def per_device(sources, labels):
    count_x, count_y, length = sources.shape
    span = length // lax.axis_size(ALL)
    heat_time = (length / 8.0) ** 2
    grad_floor = 0.04 / heat_time
    scale = 1.0 / float(length) ** 3
    cas = cas_table(length)
    wave = jnp.arange(length, dtype=jnp.int32)
    wave_z = lax.axis_index(ALL) * span + jnp.arange(span, dtype=jnp.int32)
    laplace = (
        eigen(wave, length)[None, :, None] + eigen(wave, length)[None, None, :]
    ) + eigen(wave_z, length)[:, None, None]
    anchor = (wave_z[:, None, None] == 0) & (wave[None, :, None] == 0) & (wave[None, None, :] == 0)

    heat_filter = 1.0 + heat_time * laplace
    laplace_safe = jnp.where(anchor, 1.0, laplace)
    cas_x = cas_columns(length, window_positions(length, count_x, 2))
    cas_y = cas_columns(length, window_positions(length, count_y, 4))
    source = sources.astype(jnp.float32)
    spectrum = planes_forward(to_planes(source, cas), cas)
    padded = to_pencil_with_halo(spectrum / heat_filter * scale, cas, cas_x, cas_y)
    divergence = divergence_of_flow(padded[:, 2:-2], grad_floor)

    div_spectrum = planes_forward(to_planes(divergence, cas), cas)
    potential_spectrum = jnp.where(anchor, 0.0, -div_spectrum / laplace_safe) * scale
    potential = to_pencil(planes_inverse(potential_spectrum, cas), cas, count_x, count_y)
    signs = (2 * labels - 1).astype(jnp.float32)
    return signs * potential


def solution(mesh):
    return jax.shard_map(
        per_device,
        mesh=mesh,
        in_specs=(P("wide", "narrow", None), P("wide", "narrow", None)),
        out_specs=P("wide", "narrow", None),
        check_vma=False,
    )
```
